512 devices in a mesh: gx: 16 (over y, z_hi, core), gy: 32 (over z_lo, x).
Axes of the slice: x: 4, y: 4, z: 16 (z_hi: 2, z_lo: 8; z = z_hi * 8 + z_lo), core: 2. Of those that a mesh axis runs over, the one named last changes fastest.
Arguments:
- layer_input: bfloat16 [16384, 2048], P('gy', 'gx'), may hold values from -6 to 6
- project_weight: bfloat16 [2048, 3, 2048], P(None, None, 'gx'), may hold values from -0.125 to 0.125
- output_weight: bfloat16 [2048, 2048], P('gx'), may hold values from -0.5 to 0.5
- cache_entries: bfloat16 [32, 3584, 2, 2048], P('gy', None, None, 'gx'), may hold values from -400 to 400, as said below
- cached_lengths: int32 [32], replicated, may hold values from 1 to 3584, as said below
- final_gain: bfloat16 [2048], P('gx'), may hold values from 0.099609375 to 1.8984375
- head_weight: bfloat16 [76032, 2048], P('gy', 'gx'), may hold values from -0.125 to 0.125
Outputs:
- layer_output: bfloat16 [16384, 2048], P('gy', 'gx')
- appended_entries: bfloat16 [16384, 2, 2048], P('gy', None, 'gx')
- logit_scale: float32 [32], P('gx')
- logit_peak: float32 [32], P('gx')
The draws below stay inside these ranges and needn't reach their ends.
Inputs may be any that keep to these rules, and one draw needn't show every extreme that they name: `cached_lengths`: every request has one cached slot or more; in every draw one request uses all 3584 slots and another exactly one. `cache_entries`: slots at or beyond a request's cached length are never read.
All inputs are finite; a program needn't handle non-finite values.
Results may differ from the reference program's by a relative error of at most 0.015.
Values may be sent and summed in bfloat16 or wider, within the bound.
No kernel may reach another device: no remote copies, remote signals or barrier semaphores. Data moves between devices by JAX's collectives and lax.ppermute only.
A program may use at most 64 MiB of HBM per device.

```python
import jax
import jax.numpy as jnp
from jax import lax

D = 2048
HEADS = 16
HEAD_DIM = 128
VOCAB = 76032
NEW = 512
CACHE = 3584
REQUESTS = 32
TOKENS = 16384
N_GX = 16


def draw_cache_entries(key, part):
    full_shape = (REQUESTS, CACHE, 2, HEADS * HEAD_DIM)
    scaling = jnp.array([2.0, 1.0], jnp.float32)[None, None, :, None]
    entries = jnp.clip(jax.random.normal(key, full_shape, jnp.float32), -6.0, 6.0) * scaling
    return entries.astype(jnp.bfloat16)


def draw_cached_lengths(key, part):
    lengths = jax.random.randint(key, (REQUESTS,), 1, CACHE + 1)
    longest = jax.random.randint(jax.random.fold_in(key, 5), (), 0, REQUESTS)
    places = jnp.arange(REQUESTS)
    lengths = jnp.where(places == longest, CACHE, lengths)
    lengths = jnp.where(places == (longest + 1) % REQUESTS, 1, lengths)
    return lengths.astype(jnp.int32)


def shard_levels(rng, shape, shards, least, largest):
    def one(axis_at, shards_of):
        steps = jax.random.uniform(jax.random.fold_in(jax.random.fold_in(rng, 6), axis_at), (shards_of,), jnp.float32, least / len(shards), largest / len(shards))
        return jnp.repeat(jnp.exp(steps), shape[axis_at] // shards_of).reshape((-1,) + (1,) * (len(shape) - axis_at - 1))

    gain = one(*shards[0])
    for cut in shards[1:]:
        gain = gain * one(*cut)
    return gain


def scatter_about(key, shape, deviation, bound, shards=(), kind=jnp.bfloat16):
    gain = shard_levels(key, shape, shards, -0.22, 0.18) if shards else 1.0
    result = jax.random.normal(key, shape, jnp.float32) * deviation * gain
    return jnp.minimum(jnp.maximum(result, -bound), bound).astype(kind)


def setup_inputs(seed: int = 0) -> dict:
    arg_keys = jax.random.split(jax.random.key(seed), 8)
    layer_input = scatter_about(arg_keys[0], (TOKENS, D), 1.0, 6.0, ((0, 32), (1, 16)))
    project_weight = scatter_about(arg_keys[1], (D, 3, HEADS * HEAD_DIM), D ** -0.5, 0.125, ((2, 16),))
    output_weight = scatter_about(arg_keys[2], (HEADS * HEAD_DIM, D), HEAD_DIM ** -0.5, 0.5, ((0, 16),))
    cache_entries = draw_cache_entries(jax.random.fold_in(arg_keys[7], 71), 0)
    cached_lengths = draw_cached_lengths(jax.random.fold_in(arg_keys[7], 71), 0)
    final_gain = jnp.clip(1.0 + 0.18 * jax.random.normal(arg_keys[5], (D,), jnp.float32), 0.099609375, 1.8984375).astype(jnp.bfloat16)
    head_weight = scatter_about(arg_keys[6], (VOCAB, D), D ** -0.5, 0.125, ((0, 32), (1, 16)))
    return dict(layer_input=layer_input, project_weight=project_weight, output_weight=output_weight, cache_entries=cache_entries, cached_lengths=cached_lengths, final_gain=final_gain, head_weight=head_weight)


NEG_FILL = -1e+30

def reference(layer_input, project_weight, output_weight, cache_entries, cached_lengths, final_gain, head_weight):
    model_cols = HEADS * HEAD_DIM
    group_width = model_cols // N_GX

    def one_request(packed):
        token_rows, entries, length = packed
        widened = token_rows.astype(jnp.float32)
        normed = (widened * lax.rsqrt(lax.optimization_barrier(jnp.mean(widened * widened, axis=1, keepdims=True)) + 1e-06)).astype(jnp.bfloat16)
        projected = jnp.einsum('td,dcf->tcf', normed.astype(jnp.float32), project_weight.astype(jnp.float32)).astype(jnp.bfloat16)
        queries = projected[:, 0].reshape(NEW, HEADS, HEAD_DIM)
        all_keys = jnp.concatenate([entries[:, 0], projected[:, 1]], axis=0).reshape(CACHE + NEW, HEADS, HEAD_DIM)
        all_values = jnp.concatenate([entries[:, 1], projected[:, 2]], axis=0).reshape(CACHE + NEW, HEADS, HEAD_DIM)
        scores = jnp.einsum('qhd,khd->hqk', queries.astype(jnp.float32), all_keys.astype(jnp.float32)) * HEAD_DIM ** (-0.5)
        slot_index = jnp.arange(CACHE + NEW, dtype=jnp.int32)[None, :]
        query_place = jnp.arange(NEW, dtype=jnp.int32)[:, None]
        allowed = jnp.where(slot_index < CACHE, slot_index < length, slot_index - CACHE <= query_place)
        scores = jnp.where(allowed[None], scores, NEG_FILL)
        row_max = lax.optimization_barrier(jnp.max(scores, axis=2, keepdims=True))
        weights = jnp.where(allowed[None], jnp.exp(scores - row_max), 0.0)
        mass_sum = lax.optimization_barrier(jnp.sum(weights, axis=2))
        attended = jnp.einsum('hqk,khd->hqd', weights, all_values.astype(jnp.float32), precision=lax.Precision.HIGHEST) / mass_sum[:, :, None]
        attended = jnp.transpose(attended.astype(jnp.bfloat16), (1, 0, 2)).reshape(NEW, model_cols)
        branch_sum = jnp.zeros((NEW, D), jnp.float32)
        for group_index in range(N_GX):
            lower = group_index * group_width
            group_term = jnp.dot(attended[:, lower:lower + group_width], output_weight[lower:lower + group_width], preferred_element_type=jnp.float32)
            branch_sum = branch_sum + lax.optimization_barrier(group_term.astype(jnp.bfloat16)).astype(jnp.float32)
        output_rows = (widened + branch_sum).astype(jnp.bfloat16)
        return (output_rows, projected[:, 1:3])
    per_request = layer_input.reshape(REQUESTS, NEW, D)
    outputs, appended = lax.map(one_request, (per_request, cache_entries, cached_lengths))
    last_rows = outputs[:, NEW - 1].astype(jnp.float32)
    squares = lax.optimization_barrier(jnp.sum(last_rows * last_rows, axis=1))
    gained = (last_rows * final_gain.astype(jnp.float32)).astype(jnp.bfloat16)
    logits = jnp.dot(gained, head_weight.T, preferred_element_type=jnp.float32) * lax.rsqrt(squares / D + 1e-06)[:, None]
    logit_scale = jnp.sqrt(lax.optimization_barrier(jnp.mean(logits * logits, axis=1)))
    logit_peak = lax.optimization_barrier(jnp.max(logits, axis=1))
    return (outputs.reshape(TOKENS, D), appended.reshape(TOKENS, 2, model_cols), logit_scale, logit_peak)
```

```python
import jax
import jax.numpy as jnp
import numpy as np
from jax import lax
from jax.sharding import Mesh
from jax.sharding import PartitionSpec as P

D = 2048
HEAD_DIM = 128
VOCAB = 76032

NEG_FILL = -1e30

GX = ("y", "zh", "c")
GY = ("zl", "x")


def fold_scores(carried, queries, key_block, value_block, allowed):
    running_max, mass_sum, weighted = carried
    scores = jnp.einsum(
        "qhd,khd->hqk", queries, key_block, preferred_element_type=jnp.float32
    ) * HEAD_DIM ** (-0.5)
    scores = jnp.where(allowed, scores, NEG_FILL)
    new_max = jnp.maximum(running_max, jnp.max(scores, axis=2))
    weights = jnp.where(allowed, jnp.exp(scores - new_max[:, :, None]), 0.0)
    factor = jnp.exp(running_max - new_max)
    mass_sum = mass_sum * factor + jnp.sum(weights, axis=2)
    weighted = weighted * factor[:, :, None] + jnp.einsum(
        "hqk,khd->hqd", weights, value_block.astype(jnp.float32), precision=lax.Precision.HIGHEST
    )
    return (new_max, mass_sum, weighted)


def cache_pass(queries, cache_part, live_slots, block_rows):
    query_rows, head_count, head_width = queries.shape
    block_count = cache_part.shape[0] // block_rows
    initial = (
        jnp.full((head_count, query_rows), NEG_FILL, jnp.float32),
        jnp.zeros((head_count, query_rows), jnp.float32),
        jnp.zeros((head_count, query_rows, head_width), jnp.float32),
    )

    def advance(block_index, carried):
        cache_piece = lax.dynamic_slice_in_dim(cache_part, block_index * block_rows, block_rows, 0)
        key_block = cache_piece[:, 0].reshape(block_rows, head_count, head_width)
        value_block = cache_piece[:, 1].reshape(block_rows, head_count, head_width)
        places = block_index * block_rows + jnp.arange(block_rows, dtype=jnp.int32)
        allowed = (places < live_slots)[None, None, :]
        return fold_scores(carried, queries, key_block, value_block, allowed)

    return lax.fori_loop(0, block_count, advance, initial)


def last_token_attention(query, cache_local, live_slots, new_keys, new_values):
    slots, head_count, head_width = cache_local.shape[0], query.shape[1], query.shape[2]
    cache_keys = cache_local[:, 0].reshape(slots, head_count, head_width)
    cache_values = cache_local[:, 1].reshape(slots, head_count, head_width)
    scale = HEAD_DIM ** (-0.5)
    cache_scores = jnp.einsum("qhd,khd->hqk", query, cache_keys, preferred_element_type=jnp.float32) * scale
    new_scores = jnp.einsum("qhd,khd->hqk", query, new_keys, preferred_element_type=jnp.float32) * scale
    live = (jnp.arange(slots, dtype=jnp.int32) < live_slots)[None, None, :]
    cache_scores = jnp.where(live, cache_scores, NEG_FILL)
    row_max = jnp.maximum(jnp.max(cache_scores, axis=2), jnp.max(new_scores, axis=2))
    cache_weights = jnp.where(live, jnp.exp(cache_scores - row_max[:, :, None]), 0.0)
    new_weights = jnp.exp(new_scores - row_max[:, :, None])
    mass = jnp.sum(cache_weights, axis=2) + jnp.sum(new_weights, axis=2)
    total = jnp.einsum(
        "hqk,khd->hqd", cache_weights, cache_values.astype(jnp.float32), precision=lax.Precision.HIGHEST
    ) + jnp.einsum(
        "hqk,khd->hqd", new_weights, new_values.astype(jnp.float32), precision=lax.Precision.HIGHEST
    )
    return (total / mass[:, :, None]).astype(jnp.bfloat16)


def per_device(
    layer_input,
    project_weight,
    output_weight,
    cache_entries,
    cached_lengths,
    final_gain,
    head_weight,
):
    new_rows, block_cols = layer_input.shape
    n_y, n_zh, n_c = lax.axis_size("y"), lax.axis_size("zh"), lax.axis_size("c")
    n_gx = n_y * n_zh * n_c
    n_gy = lax.axis_size("zl") * lax.axis_size("x")
    head_count = output_weight.shape[0] // HEAD_DIM
    request = lax.axis_index("zl") * lax.axis_size("x") + lax.axis_index("x")
    own_len = lax.dynamic_index_in_dim(cached_lengths, request, 0, keepdims=False)

    pair = lax.all_gather(layer_input, "zh", axis=1, tiled=True)
    features = lax.all_gather(pair, ("y", "c"), axis=1, tiled=True)
    weight_rows = project_weight.reshape(n_y, n_zh, n_c, block_cols, 3, project_weight.shape[-1])
    weight_rows = jnp.transpose(weight_rows, (0, 2, 1, 3, 4, 5)).reshape(project_weight.shape)

    widened = features.astype(jnp.float32)
    normed = (
        widened * lax.rsqrt(jnp.mean(widened * widened, axis=1, keepdims=True) + 1e-06)
    ).astype(jnp.bfloat16)
    projected = jnp.einsum(
        "td,dcf->tcf", normed, weight_rows, preferred_element_type=jnp.float32
    )
    rounded = projected.astype(jnp.bfloat16)
    queries = rounded[:, 0].reshape(new_rows, head_count, HEAD_DIM)
    new_keys = rounded[:, 1].reshape(new_rows, head_count, HEAD_DIM)
    new_values = rounded[:, 2].reshape(new_rows, head_count, HEAD_DIM)
    appended = rounded[:, 1:3]
    cache_local = cache_entries[0]

    last_attended = last_token_attention(
        queries[new_rows - 1 :], cache_local, own_len, new_keys, new_values
    )
    last_attended = jnp.transpose(last_attended, (1, 0, 2)).reshape(1, head_count * HEAD_DIM)
    last_term = jnp.dot(last_attended, output_weight, preferred_element_type=jnp.float32)
    last_term = last_term.astype(jnp.bfloat16).reshape(n_gx, block_cols)
    last_terms = lax.all_to_all(last_term, GX, 0, 0, tiled=True)
    last_row = (
        layer_input[new_rows - 1].astype(jnp.float32) + jnp.sum(last_terms.astype(jnp.float32), axis=0)
    ).astype(jnp.bfloat16)
    every_last = lax.all_to_all(
        jnp.broadcast_to(last_row[None], (n_gy, block_cols)), GY, 0, 0, tiled=True
    )
    last_wide = every_last.astype(jnp.float32)
    square_part = jnp.sum(last_wide * last_wide, axis=1, keepdims=True)
    gained = (last_wide * final_gain.astype(jnp.float32)).astype(jnp.bfloat16)
    logit_part = jnp.einsum("rd,vd->rv", gained, head_weight, preferred_element_type=jnp.float32)
    packed = jnp.concatenate([logit_part, square_part], axis=1)
    packed = lax.all_to_all(packed, GX, 0, 0, tiled=True)
    own_requests = packed.shape[0] // n_gx
    packed = jnp.sum(packed.reshape(n_gx, own_requests, packed.shape[1]), axis=0)
    vocab_part = logit_part.shape[1]
    logits = packed[:, :vocab_part] * lax.rsqrt(packed[:, vocab_part:] / D + 1e-06)
    stats = jnp.stack([jnp.sum(logits * logits, axis=1), jnp.max(logits, axis=1)], axis=0)
    stats = lax.all_to_all(
        jnp.broadcast_to(stats[None], (n_gy,) + stats.shape), GY, 0, 0, tiled=True
    )
    logit_scale = jnp.sqrt(jnp.sum(stats[:, 0], axis=0) / VOCAB)
    logit_peak = jnp.max(stats[:, 1], axis=0)

    cache_slots = cache_local.shape[0]
    block_rows = min(256, cache_slots // 2)
    carried = cache_pass(queries, cache_local, own_len, block_rows)
    causal = (jnp.arange(new_rows)[None, :] <= jnp.arange(new_rows)[:, None])[None]
    carried = fold_scores(carried, queries, new_keys, new_values, causal)
    attended = (carried[2] / carried[1][:, :, None]).astype(jnp.bfloat16)
    attended = jnp.transpose(attended, (1, 0, 2)).reshape(new_rows, head_count * HEAD_DIM)
    out_cols = output_weight.reshape(-1, n_y, n_zh, n_c, block_cols)
    out_cols = jnp.transpose(out_cols, (0, 1, 3, 2, 4)).reshape(output_weight.shape)
    partial_out = jnp.dot(attended, out_cols, preferred_element_type=jnp.float32).astype(jnp.bfloat16)
    branch = lax.psum_scatter(partial_out, ("y", "c"), scatter_dimension=1, tiled=True)
    branch = lax.psum_scatter(branch, "zh", scatter_dimension=1, tiled=True)
    layer_output = (layer_input.astype(jnp.float32) + branch.astype(jnp.float32)).astype(jnp.bfloat16)
    return (layer_output, appended, logit_scale, logit_peak)


def solution(mesh):
    devices = np.asarray(mesh.devices)
    n_gx, n_gy = devices.shape
    fine = Mesh(devices.reshape(n_gx // 4, 2, 2, n_gy // 4, 4), GX + GY)
    return jax.shard_map(
        per_device,
        mesh=fine,
        in_specs=(
            P(GY, GX),
            P(None, None, GX),
            P(GX, None),
            P(GY, None, None, GX),
            P(),
            P(GX),
            P(GY, GX),
        ),
        out_specs=(P(GY, GX), P(GY, None, GX), P(GX), P(GX)),
        check_vma=False,
    )
```

```python
import jax
import jax.numpy as jnp
import numpy as np
from jax import lax
from jax.sharding import Mesh
from jax.sharding import PartitionSpec as P

D = 2048
HEAD_DIM = 128
VOCAB = 76032

NEG_FILL = -1e30

GX = ("y", "zh", "c")
GY = ("zl", "x")


def fold_scores(carried, queries, key_block, value_block, allowed):
    running_max, mass_sum, weighted = carried
    scores = jnp.einsum(
        "qhd,khd->hqk", queries, key_block, preferred_element_type=jnp.float32
    ) * HEAD_DIM ** (-0.5)
    scores = jnp.where(allowed, scores, NEG_FILL)
    new_max = jnp.maximum(running_max, jnp.max(scores, axis=2))
    weights = jnp.where(allowed, jnp.exp(scores - new_max[:, :, None]), 0.0)
    factor = jnp.exp(running_max - new_max)
    mass_sum = mass_sum * factor + jnp.sum(weights, axis=2)
    weighted = weighted * factor[:, :, None] + jnp.einsum(
        "hqk,khd->hqd", weights, value_block.astype(jnp.float32), precision=lax.Precision.HIGHEST
    )
    return (new_max, mass_sum, weighted)


def cache_pass(queries, cache_part, live_slots, block_rows):
    query_rows, head_count, head_width = queries.shape
    block_count = cache_part.shape[0] // block_rows
    initial = (
        jnp.full((head_count, query_rows), NEG_FILL, jnp.float32),
        jnp.zeros((head_count, query_rows), jnp.float32),
        jnp.zeros((head_count, query_rows, head_width), jnp.float32),
    )

    def advance(block_index, carried):
        cache_piece = lax.dynamic_slice_in_dim(cache_part, block_index * block_rows, block_rows, 0)
        key_block = cache_piece[:, 0].reshape(block_rows, head_count, head_width)
        value_block = cache_piece[:, 1].reshape(block_rows, head_count, head_width)
        places = block_index * block_rows + jnp.arange(block_rows, dtype=jnp.int32)
        allowed = (places < live_slots)[None, None, :]
        return fold_scores(carried, queries, key_block, value_block, allowed)

    return lax.fori_loop(0, block_count, advance, initial)


def last_token_attention(query, cache_local, live_slots, new_keys, new_values):
    slots, head_count, head_width = cache_local.shape[0], query.shape[1], query.shape[2]
    cache_keys = cache_local[:, 0].reshape(slots, head_count, head_width)
    cache_values = cache_local[:, 1].reshape(slots, head_count, head_width)
    scale = HEAD_DIM ** (-0.5)
    cache_scores = jnp.einsum("qhd,khd->hqk", query, cache_keys, preferred_element_type=jnp.float32) * scale
    new_scores = jnp.einsum("qhd,khd->hqk", query, new_keys, preferred_element_type=jnp.float32) * scale
    live = (jnp.arange(slots, dtype=jnp.int32) < live_slots)[None, None, :]
    cache_scores = jnp.where(live, cache_scores, NEG_FILL)
    row_max = jnp.maximum(jnp.max(cache_scores, axis=2), jnp.max(new_scores, axis=2))
    cache_weights = jnp.where(live, jnp.exp(cache_scores - row_max[:, :, None]), 0.0)
    new_weights = jnp.exp(new_scores - row_max[:, :, None])
    mass = jnp.sum(cache_weights, axis=2) + jnp.sum(new_weights, axis=2)
    total = jnp.einsum(
        "hqk,khd->hqd", cache_weights, cache_values.astype(jnp.float32), precision=lax.Precision.HIGHEST
    ) + jnp.einsum(
        "hqk,khd->hqd", new_weights, new_values.astype(jnp.float32), precision=lax.Precision.HIGHEST
    )
    return (total / mass[:, :, None]).astype(jnp.bfloat16)


def per_device(
    layer_input,
    project_weight,
    output_weight,
    cache_entries,
    cached_lengths,
    final_gain,
    head_weight,
):
    new_rows, block_cols = layer_input.shape
    n_y, n_zh, n_c = lax.axis_size("y"), lax.axis_size("zh"), lax.axis_size("c")
    n_gx = n_y * n_zh * n_c
    n_gy = lax.axis_size("zl") * lax.axis_size("x")
    head_count = output_weight.shape[0] // HEAD_DIM
    request = lax.axis_index("zl") * lax.axis_size("x") + lax.axis_index("x")
    own_len = lax.dynamic_index_in_dim(cached_lengths, request, 0, keepdims=False)

    pair = lax.all_gather(layer_input, "zh", axis=1, tiled=True)
    features = lax.all_gather(pair, ("y", "c"), axis=1, tiled=True)
    weight_rows = project_weight.reshape(n_y, n_zh, n_c, block_cols, 3, project_weight.shape[-1])
    weight_rows = jnp.transpose(weight_rows, (0, 2, 1, 3, 4, 5)).reshape(project_weight.shape)

    widened = features.astype(jnp.float32)
    normed = (
        widened * lax.rsqrt(jnp.mean(widened * widened, axis=1, keepdims=True) + 1e-06)
    ).astype(jnp.bfloat16)
    projected = jnp.einsum(
        "td,dcf->tcf", normed, weight_rows, preferred_element_type=jnp.float32
    )
    rounded = projected.astype(jnp.bfloat16)
    queries = rounded[:, 0].reshape(new_rows, head_count, HEAD_DIM)
    new_keys = rounded[:, 1].reshape(new_rows, head_count, HEAD_DIM)
    new_values = rounded[:, 2].reshape(new_rows, head_count, HEAD_DIM)
    appended = rounded[:, 1:3]
    cache_local = cache_entries[0]

    out_cols = output_weight.reshape(-1, n_y, n_zh, n_c, block_cols)
    out_cols = jnp.transpose(out_cols, (0, 1, 3, 2, 4)).reshape(output_weight.shape)

    cache_slots = cache_local.shape[0]
    block_rows = min(256, cache_slots // 2)
    carried = cache_pass(queries, cache_local, own_len, block_rows)
    causal = (jnp.arange(new_rows)[None, :] <= jnp.arange(new_rows)[:, None])[None]
    carried = fold_scores(carried, queries, new_keys, new_values, causal)
    attended = (carried[2] / carried[1][:, :, None]).astype(jnp.bfloat16)
    attended = jnp.transpose(attended, (1, 0, 2)).reshape(new_rows, head_count * HEAD_DIM)
    partial_out = jnp.dot(attended, out_cols, preferred_element_type=jnp.float32).astype(jnp.bfloat16)
    branch = lax.psum_scatter(partial_out, ("y", "c"), scatter_dimension=1, tiled=True)
    last_attended = last_token_attention(
        queries[new_rows - 1 :], cache_local, own_len, new_keys, new_values
    )
    last_attended = jnp.transpose(last_attended, (1, 0, 2)).reshape(1, head_count * HEAD_DIM)
    last_term = jnp.dot(last_attended, out_cols, preferred_element_type=jnp.float32)
    last_term = last_term.astype(jnp.bfloat16).reshape(n_y, n_c, n_zh, block_cols)
    last_term = jnp.transpose(last_term, (0, 2, 1, 3)).reshape(n_gx, block_cols)
    last_terms = lax.all_to_all(last_term, GX, 0, 0, tiled=True)
    last_row = (
        layer_input[new_rows - 1].astype(jnp.float32) + jnp.sum(last_terms.astype(jnp.float32), axis=0)
    ).astype(jnp.bfloat16)
    every_last = lax.all_to_all(
        jnp.broadcast_to(last_row[None], (n_gy, block_cols)), GY, 0, 0, tiled=True
    )
    last_wide = every_last.astype(jnp.float32)
    square_part = jnp.sum(last_wide * last_wide, axis=1, keepdims=True)
    gained = (last_wide * final_gain.astype(jnp.float32)).astype(jnp.bfloat16)
    logit_part = jnp.einsum("rd,vd->rv", gained, head_weight, preferred_element_type=jnp.float32)
    packed = jnp.concatenate([logit_part, square_part], axis=1)
    packed = lax.all_to_all(packed, GX, 0, 0, tiled=True)
    own_requests = packed.shape[0] // n_gx
    packed = jnp.sum(packed.reshape(n_gx, own_requests, packed.shape[1]), axis=0)
    vocab_part = logit_part.shape[1]
    logits = packed[:, :vocab_part] * lax.rsqrt(packed[:, vocab_part:] / D + 1e-06)
    stats = jnp.stack([jnp.sum(logits * logits, axis=1), jnp.max(logits, axis=1)], axis=0)
    spread = jnp.broadcast_to(stats[None], (n_gy,) + stats.shape)
    spread, branch = lax.optimization_barrier((spread, branch))
    branch = branch.reshape(new_rows, n_zh, block_cols)
    zh = lax.axis_index("zh")
    mine = lax.dynamic_index_in_dim(branch, zh, 1, keepdims=False)
    theirs = lax.dynamic_index_in_dim(branch, 1 - zh, 1, keepdims=False)
    from_partner = lax.ppermute(theirs, "zh", [(0, 1), (1, 0)])
    stats = lax.all_to_all(spread, GY, 0, 0, tiled=True)
    logit_scale = jnp.sqrt(jnp.sum(stats[:, 0], axis=0) / VOCAB)
    logit_peak = jnp.max(stats[:, 1], axis=0)

    layer_output = (
        layer_input.astype(jnp.float32) + mine.astype(jnp.float32) + from_partner.astype(jnp.float32)
    ).astype(jnp.bfloat16)
    return (layer_output, appended, logit_scale, logit_peak)


def solution(mesh):
    devices = np.asarray(mesh.devices)
    n_gx, n_gy = devices.shape
    fine = Mesh(devices.reshape(n_gx // 4, 2, 2, n_gy // 4, 4), GX + GY)
    return jax.shard_map(
        per_device,
        mesh=fine,
        in_specs=(
            P(GY, GX),
            P(None, None, GX),
            P(GX, None),
            P(GY, None, None, GX),
            P(),
            P(GX),
            P(GY, GX),
        ),
        out_specs=(P(GY, GX), P(GY, None, GX), P(GX), P(GX)),
        check_vma=False,
    )
```

```python
import jax
import jax.numpy as jnp
import numpy as np
from jax import lax
from jax.sharding import Mesh
from jax.sharding import PartitionSpec as P

D = 2048
HEAD_DIM = 128
VOCAB = 76032

NEG_FILL = -1e30

GX = ("y", "zh", "c")
GY = ("zl", "x")


def fold_scores(carried, queries, key_block, value_block, allowed):
    running_max, mass_sum, weighted = carried
    scores = jnp.einsum(
        "qhd,khd->hqk", queries, key_block, preferred_element_type=jnp.float32
    ) * HEAD_DIM ** (-0.5)
    scores = jnp.where(allowed, scores, NEG_FILL)
    new_max = jnp.maximum(running_max, jnp.max(scores, axis=2))
    weights = jnp.where(allowed, jnp.exp(scores - new_max[:, :, None]), 0.0)
    factor = jnp.exp(running_max - new_max)
    mass_sum = mass_sum * factor + jnp.sum(weights, axis=2)
    weighted = weighted * factor[:, :, None] + jnp.einsum(
        "hqk,khd->hqd", weights, value_block.astype(jnp.float32), precision=lax.Precision.HIGHEST
    )
    return (new_max, mass_sum, weighted)


def cache_pass(queries, cache_part, live_slots, block_rows):
    query_rows, head_count, head_width = queries.shape
    block_count = cache_part.shape[0] // block_rows
    initial = (
        jnp.full((head_count, query_rows), NEG_FILL, jnp.float32),
        jnp.zeros((head_count, query_rows), jnp.float32),
        jnp.zeros((head_count, query_rows, head_width), jnp.float32),
    )

    def advance(block_index, carried):
        cache_piece = lax.dynamic_slice_in_dim(cache_part, block_index * block_rows, block_rows, 0)
        key_block = cache_piece[:, 0].reshape(block_rows, head_count, head_width)
        value_block = cache_piece[:, 1].reshape(block_rows, head_count, head_width)
        places = block_index * block_rows + jnp.arange(block_rows, dtype=jnp.int32)
        allowed = (places < live_slots)[None, None, :]
        return fold_scores(carried, queries, key_block, value_block, allowed)

    return lax.fori_loop(0, block_count, advance, initial)


def per_device(
    layer_input,
    project_weight,
    output_weight,
    cache_entries,
    cached_lengths,
    final_gain,
    head_weight,
):
    new_rows, block_cols = layer_input.shape
    n_y, n_zh, n_c = lax.axis_size("y"), lax.axis_size("zh"), lax.axis_size("c")
    n_gx = n_y * n_zh * n_c
    n_gy = lax.axis_size("zl") * lax.axis_size("x")
    head_count = output_weight.shape[0] // HEAD_DIM
    request = lax.axis_index("zl") * lax.axis_size("x") + lax.axis_index("x")
    own_len = lax.dynamic_index_in_dim(cached_lengths, request, 0, keepdims=False)

    pair = lax.all_gather(layer_input, "zh", axis=1, tiled=True)
    features = lax.all_gather(pair, ("y", "c"), axis=1, tiled=True)
    weight_rows = project_weight.reshape(n_y, n_zh, n_c, block_cols, 3, project_weight.shape[-1])
    weight_rows = jnp.transpose(weight_rows, (0, 2, 1, 3, 4, 5)).reshape(project_weight.shape)

    widened = features.astype(jnp.float32)
    normed = (
        widened * lax.rsqrt(jnp.mean(widened * widened, axis=1, keepdims=True) + 1e-06)
    ).astype(jnp.bfloat16)
    projected = jnp.einsum(
        "td,dcf->tcf", normed, weight_rows, preferred_element_type=jnp.float32
    )
    rounded = projected.astype(jnp.bfloat16)
    queries = rounded[:, 0].reshape(new_rows, head_count, HEAD_DIM)
    new_keys = rounded[:, 1].reshape(new_rows, head_count, HEAD_DIM)
    new_values = rounded[:, 2].reshape(new_rows, head_count, HEAD_DIM)
    appended = rounded[:, 1:3]
    cache_local = cache_entries[0]

    out_cols = output_weight.reshape(-1, n_y, n_zh, n_c, block_cols)
    out_cols = jnp.transpose(out_cols, (0, 1, 3, 2, 4)).reshape(output_weight.shape)

    cache_slots = cache_local.shape[0]
    block_rows = min(256, cache_slots // 2)
    carried = cache_pass(queries, cache_local, own_len, block_rows)
    causal = (jnp.arange(new_rows)[None, :] <= jnp.arange(new_rows)[:, None])[None]
    carried = fold_scores(carried, queries, new_keys, new_values, causal)
    attended = (carried[2] / carried[1][:, :, None]).astype(jnp.bfloat16)
    attended = jnp.transpose(attended, (1, 0, 2)).reshape(new_rows, head_count * HEAD_DIM)
    partial_out = jnp.dot(attended, out_cols, preferred_element_type=jnp.float32).astype(jnp.bfloat16)
    branch = lax.psum_scatter(partial_out, ("y", "c"), scatter_dimension=1, tiled=True)
    last_term = partial_out[new_rows - 1].reshape(n_y, n_c, n_zh, block_cols)
    last_term = jnp.transpose(last_term, (0, 2, 1, 3)).reshape(n_gx, block_cols)
    last_terms = lax.all_to_all(last_term, GX, 0, 0, tiled=True)
    last_row = (
        layer_input[new_rows - 1].astype(jnp.float32) + jnp.sum(last_terms.astype(jnp.float32), axis=0)
    ).astype(jnp.bfloat16)
    every_last = lax.all_to_all(
        jnp.broadcast_to(last_row[None], (n_gy, block_cols)), GY, 0, 0, tiled=True
    )
    last_wide = every_last.astype(jnp.float32)
    square_part = jnp.sum(last_wide * last_wide, axis=1, keepdims=True)
    gained = (last_wide * final_gain.astype(jnp.float32)).astype(jnp.bfloat16)
    logit_part = jnp.einsum("rd,vd->rv", gained, head_weight, preferred_element_type=jnp.float32)
    packed = jnp.concatenate([logit_part, square_part], axis=1)
    packed, branch = lax.optimization_barrier((packed, branch))
    branch = branch.reshape(new_rows, n_zh, block_cols)
    zh = lax.axis_index("zh")
    mine = lax.dynamic_index_in_dim(branch, zh, 1, keepdims=False)
    theirs = lax.dynamic_index_in_dim(branch, 1 - zh, 1, keepdims=False)
    from_partner = lax.ppermute(theirs, "zh", [(0, 1), (1, 0)])
    packed = lax.all_to_all(packed, GX, 0, 0, tiled=True)
    own_requests = packed.shape[0] // n_gx
    packed = jnp.sum(packed.reshape(n_gx, own_requests, packed.shape[1]), axis=0)
    vocab_part = logit_part.shape[1]
    logits = packed[:, :vocab_part] * lax.rsqrt(packed[:, vocab_part:] / D + 1e-06)
    stats = jnp.stack([jnp.sum(logits * logits, axis=1), jnp.max(logits, axis=1)], axis=0)
    spread = jnp.broadcast_to(stats[None], (n_gy,) + stats.shape)
    stats = lax.all_to_all(spread, GY, 0, 0, tiled=True)
    logit_scale = jnp.sqrt(jnp.sum(stats[:, 0], axis=0) / VOCAB)
    logit_peak = jnp.max(stats[:, 1], axis=0)

    layer_output = (
        layer_input.astype(jnp.float32) + mine.astype(jnp.float32) + from_partner.astype(jnp.float32)
    ).astype(jnp.bfloat16)
    return (layer_output, appended, logit_scale, logit_peak)


def solution(mesh):
    devices = np.asarray(mesh.devices)
    n_gx, n_gy = devices.shape
    fine = Mesh(devices.reshape(n_gx // 4, 2, 2, n_gy // 4, 4), GX + GY)
    return jax.shard_map(
        per_device,
        mesh=fine,
        in_specs=(
            P(GY, GX),
            P(None, None, GX),
            P(GX, None),
            P(GY, None, None, GX),
            P(),
            P(GX),
            P(GY, GX),
        ),
        out_specs=(P(GY, GX), P(GY, None, GX), P(GX), P(GX)),
        check_vma=False,
    )
```

```python
import jax
import jax.numpy as jnp
import numpy as np
from jax import lax
from jax.sharding import Mesh
from jax.sharding import PartitionSpec as P

D = 2048
HEAD_DIM = 128
VOCAB = 76032

NEG_FILL = -1e30

GX = ("y", "zh", "c")
GY = ("zl", "x")


def fold_scores(carried, queries, key_block, value_block, allowed):
    running_max, mass_sum, weighted = carried
    scores = jnp.einsum(
        "qhd,khd->hqk", queries, key_block, preferred_element_type=jnp.float32
    ) * HEAD_DIM ** (-0.5)
    scores = jnp.where(allowed, scores, NEG_FILL)
    new_max = jnp.maximum(running_max, jnp.max(scores, axis=2))
    weights = jnp.where(allowed, jnp.exp(scores - new_max[:, :, None]), 0.0)
    factor = jnp.exp(running_max - new_max)
    mass_sum = mass_sum * factor + jnp.sum(weights, axis=2)
    high = weights.astype(jnp.bfloat16)
    low = (weights - high.astype(jnp.float32)).astype(jnp.bfloat16)
    weighted = weighted * factor[:, :, None] + (
        jnp.einsum("hqk,khd->hqd", high, value_block, preferred_element_type=jnp.float32)
        + jnp.einsum("hqk,khd->hqd", low, value_block, preferred_element_type=jnp.float32)
    )
    return (new_max, mass_sum, weighted)


def cache_pass(queries, cache_part, live_slots, block_rows):
    query_rows, head_count, head_width = queries.shape
    block_count = cache_part.shape[0] // block_rows
    initial = (
        jnp.full((head_count, query_rows), NEG_FILL, jnp.float32),
        jnp.zeros((head_count, query_rows), jnp.float32),
        jnp.zeros((head_count, query_rows, head_width), jnp.float32),
    )

    def advance(block_index, carried):
        cache_piece = lax.dynamic_slice_in_dim(cache_part, block_index * block_rows, block_rows, 0)
        key_block = cache_piece[:, 0].reshape(block_rows, head_count, head_width)
        value_block = cache_piece[:, 1].reshape(block_rows, head_count, head_width)
        places = block_index * block_rows + jnp.arange(block_rows, dtype=jnp.int32)
        allowed = (places < live_slots)[None, None, :]
        return fold_scores(carried, queries, key_block, value_block, allowed)

    return lax.fori_loop(0, block_count, advance, initial)


def per_device(
    layer_input,
    project_weight,
    output_weight,
    cache_entries,
    cached_lengths,
    final_gain,
    head_weight,
):
    new_rows, block_cols = layer_input.shape
    n_y, n_zh, n_c = lax.axis_size("y"), lax.axis_size("zh"), lax.axis_size("c")
    n_gx = n_y * n_zh * n_c
    n_gy = lax.axis_size("zl") * lax.axis_size("x")
    head_count = output_weight.shape[0] // HEAD_DIM
    request = lax.axis_index("zl") * lax.axis_size("x") + lax.axis_index("x")
    own_len = lax.dynamic_index_in_dim(cached_lengths, request, 0, keepdims=False)

    pair = lax.all_gather(layer_input, "zh", axis=1, tiled=True)
    features = lax.all_gather(pair, ("y", "c"), axis=1, tiled=True)
    weight_rows = project_weight.reshape(n_y, n_zh, n_c, block_cols, 3, project_weight.shape[-1])
    weight_rows = jnp.transpose(weight_rows, (0, 2, 1, 3, 4, 5)).reshape(project_weight.shape)

    widened = features.astype(jnp.float32)
    normed = (
        widened * lax.rsqrt(jnp.mean(widened * widened, axis=1, keepdims=True) + 1e-06)
    ).astype(jnp.bfloat16)
    projected = jnp.einsum(
        "td,dcf->tcf", normed, weight_rows, preferred_element_type=jnp.float32
    )
    rounded = projected.astype(jnp.bfloat16)
    queries = rounded[:, 0].reshape(new_rows, head_count, HEAD_DIM)
    new_keys = rounded[:, 1].reshape(new_rows, head_count, HEAD_DIM)
    new_values = rounded[:, 2].reshape(new_rows, head_count, HEAD_DIM)
    appended = rounded[:, 1:3]
    cache_local = cache_entries[0]

    out_cols = output_weight.reshape(-1, n_y, n_zh, n_c, block_cols)
    out_cols = jnp.transpose(out_cols, (0, 1, 3, 2, 4)).reshape(output_weight.shape)

    cache_slots = cache_local.shape[0]
    block_rows = min(512, cache_slots // 2)
    carried = cache_pass(queries, cache_local, own_len, block_rows)
    causal = (jnp.arange(new_rows)[None, :] <= jnp.arange(new_rows)[:, None])[None]
    carried = fold_scores(carried, queries, new_keys, new_values, causal)
    attended = (carried[2] / carried[1][:, :, None]).astype(jnp.bfloat16)
    attended = jnp.transpose(attended, (1, 0, 2)).reshape(new_rows, head_count * HEAD_DIM)
    partial_out = jnp.dot(attended, out_cols, preferred_element_type=jnp.float32).astype(jnp.bfloat16)
    branch = lax.psum_scatter(partial_out, ("y", "c"), scatter_dimension=1, tiled=True)
    last_term = partial_out[new_rows - 1].reshape(n_y, n_c, n_zh, block_cols)
    last_term = jnp.transpose(last_term, (0, 2, 1, 3)).reshape(n_gx, block_cols)
    last_terms = lax.all_to_all(last_term, GX, 0, 0, tiled=True)
    last_row = (
        layer_input[new_rows - 1].astype(jnp.float32) + jnp.sum(last_terms.astype(jnp.float32), axis=0)
    ).astype(jnp.bfloat16)
    every_last = lax.all_to_all(
        jnp.broadcast_to(last_row[None], (n_gy, block_cols)), GY, 0, 0, tiled=True
    )
    last_wide = every_last.astype(jnp.float32)
    square_part = jnp.sum(last_wide * last_wide, axis=1, keepdims=True)
    gained = (last_wide * final_gain.astype(jnp.float32)).astype(jnp.bfloat16)
    logit_part = jnp.einsum("rd,vd->rv", gained, head_weight, preferred_element_type=jnp.float32)
    packed = jnp.concatenate([logit_part, square_part], axis=1)
    packed, branch = lax.optimization_barrier((packed, branch))
    branch = branch.reshape(new_rows, n_zh, block_cols)
    zh = lax.axis_index("zh")
    mine = lax.dynamic_index_in_dim(branch, zh, 1, keepdims=False)
    theirs = lax.dynamic_index_in_dim(branch, 1 - zh, 1, keepdims=False)
    from_partner = lax.ppermute(theirs, "zh", [(0, 1), (1, 0)])
    packed = lax.all_to_all(packed, GX, 0, 0, tiled=True)
    own_requests = packed.shape[0] // n_gx
    packed = jnp.sum(packed.reshape(n_gx, own_requests, packed.shape[1]), axis=0)
    vocab_part = logit_part.shape[1]
    logits = packed[:, :vocab_part] * lax.rsqrt(packed[:, vocab_part:] / D + 1e-06)
    stats = jnp.stack([jnp.sum(logits * logits, axis=1), jnp.max(logits, axis=1)], axis=0)
    spread = jnp.broadcast_to(stats[None], (n_gy,) + stats.shape)
    stats = lax.all_to_all(spread, GY, 0, 0, tiled=True)
    logit_scale = jnp.sqrt(jnp.sum(stats[:, 0], axis=0) / VOCAB)
    logit_peak = jnp.max(stats[:, 1], axis=0)

    layer_output = (
        layer_input.astype(jnp.float32) + mine.astype(jnp.float32) + from_partner.astype(jnp.float32)
    ).astype(jnp.bfloat16)
    return (layer_output, appended, logit_scale, logit_peak)


def solution(mesh):
    devices = np.asarray(mesh.devices)
    n_gx, n_gy = devices.shape
    fine = Mesh(devices.reshape(n_gx // 4, 2, 2, n_gy // 4, 4), GX + GY)
    return jax.shard_map(
        per_device,
        mesh=fine,
        in_specs=(
            P(GY, GX),
            P(None, None, GX),
            P(GX, None),
            P(GY, None, None, GX),
            P(),
            P(GX),
            P(GY, GX),
        ),
        out_specs=(P(GY, GX), P(GY, None, GX), P(GX), P(GX)),
        check_vma=False,
    )
```

```python
import functools

import jax
import jax.numpy as jnp
import numpy as np
from jax import lax
from jax.experimental import pallas as pl
from jax.experimental.pallas import tpu as pltpu
from jax.sharding import Mesh
from jax.sharding import PartitionSpec as P

D = 2048
HEAD_DIM = 128
VOCAB = 76032

NEG_FILL = -1e30

GX = ("y", "zh", "c")
GY = ("zl", "x")


def attention_kernel(cache_slots, key_rows, len_ref, q_ref, k_ref, v_ref, o_ref, m_sc, l_sc, acc_sc):
    step = pl.program_id(0)

    @pl.when(step == 0)
    def _():
        m_sc[...] = jnp.full(m_sc.shape, NEG_FILL, jnp.float32)
        l_sc[...] = jnp.zeros(l_sc.shape, jnp.float32)
        acc_sc[...] = jnp.zeros(acc_sc.shape, jnp.float32)

    q = q_ref[...]
    k = k_ref[...]
    s = lax.dot_general(q, k, (((1,), (1,)), ((), ())), preferred_element_type=jnp.float32) * HEAD_DIM ** (-0.5)
    rows = q.shape[0]
    slot = step * key_rows + lax.broadcasted_iota(jnp.int32, (rows, key_rows), 1)
    place = lax.broadcasted_iota(jnp.int32, (rows, key_rows), 0)
    limit = jnp.where(slot < cache_slots, len_ref[0], cache_slots + place + 1)
    allowed = slot < limit
    s = jnp.where(allowed, s, NEG_FILL)
    m_old = m_sc[...]
    m_new = jnp.maximum(m_old, jnp.max(s, axis=1, keepdims=True))
    p = jnp.where(allowed, jnp.exp(s - m_new), 0.0)
    factor = jnp.exp(m_old - m_new)
    l_sc[...] = l_sc[...] * factor + jnp.sum(p, axis=1, keepdims=True)
    v = v_ref[...]
    high = p.astype(jnp.bfloat16)
    low = (p - high.astype(jnp.float32)).astype(jnp.bfloat16)
    pv = jnp.dot(high, v, preferred_element_type=jnp.float32) + jnp.dot(low, v, preferred_element_type=jnp.float32)
    acc_sc[...] = acc_sc[...] * factor + pv
    m_sc[...] = m_new

    @pl.when(step == pl.num_programs(0) - 1)
    def _():
        o_ref[...] = (acc_sc[...] / l_sc[...]).astype(o_ref.dtype)


def attend(queries, keys, values, live_slots, cache_slots, key_rows=512):
    rows, width = queries.shape
    steps = keys.shape[0] // key_rows
    return pl.pallas_call(
        functools.partial(attention_kernel, cache_slots, key_rows),
        grid_spec=pltpu.PrefetchScalarGridSpec(
            num_scalar_prefetch=1,
            grid=(steps,),
            in_specs=[
                pl.BlockSpec((rows, width), lambda i, n: (0, 0)),
                pl.BlockSpec((key_rows, width), lambda i, n: (i, 0)),
                pl.BlockSpec((key_rows, width), lambda i, n: (i, 0)),
            ],
            out_specs=pl.BlockSpec((rows, width), lambda i, n: (0, 0)),
            scratch_shapes=[
                pltpu.VMEM((rows, 1), jnp.float32),
                pltpu.VMEM((rows, 1), jnp.float32),
                pltpu.VMEM((rows, width), jnp.float32),
            ],
        ),
        out_shape=jax.ShapeDtypeStruct((rows, width), jnp.bfloat16),
        compiler_params=pltpu.CompilerParams(dimension_semantics=("arbitrary",)),
    )(live_slots, queries, keys, values)


def per_device(
    layer_input,
    project_weight,
    output_weight,
    cache_entries,
    cached_lengths,
    final_gain,
    head_weight,
):
    new_rows, block_cols = layer_input.shape
    n_y, n_zh, n_c = lax.axis_size("y"), lax.axis_size("zh"), lax.axis_size("c")
    n_gx = n_y * n_zh * n_c
    n_gy = lax.axis_size("zl") * lax.axis_size("x")
    head_count = output_weight.shape[0] // HEAD_DIM
    request = lax.axis_index("zl") * lax.axis_size("x") + lax.axis_index("x")
    own_len = lax.dynamic_index_in_dim(cached_lengths, request, 0, keepdims=False)

    pair = lax.all_gather(layer_input, "zh", axis=1, tiled=True)
    features = lax.all_gather(pair, ("y", "c"), axis=1, tiled=True)
    weight_rows = project_weight.reshape(n_y, n_zh, n_c, block_cols, 3, project_weight.shape[-1])
    weight_rows = jnp.transpose(weight_rows, (0, 2, 1, 3, 4, 5)).reshape(project_weight.shape)

    widened = features.astype(jnp.float32)
    normed = (
        widened * lax.rsqrt(jnp.mean(widened * widened, axis=1, keepdims=True) + 1e-06)
    ).astype(jnp.bfloat16)
    projected = jnp.einsum(
        "td,dcf->tcf", normed, weight_rows, preferred_element_type=jnp.float32
    )
    rounded = projected.astype(jnp.bfloat16)
    queries = rounded[:, 0].reshape(new_rows, head_count, HEAD_DIM)
    new_keys = rounded[:, 1].reshape(new_rows, head_count, HEAD_DIM)
    new_values = rounded[:, 2].reshape(new_rows, head_count, HEAD_DIM)
    appended = rounded[:, 1:3]
    cache_local = cache_entries[0]

    out_cols = output_weight.reshape(-1, n_y, n_zh, n_c, block_cols)
    out_cols = jnp.transpose(out_cols, (0, 1, 3, 2, 4)).reshape(output_weight.shape)

    cache_slots = cache_local.shape[0]
    live = jnp.reshape(own_len, (1,)).astype(jnp.int32)
    heads = []
    for h in range(head_count):
        cols = slice(h * HEAD_DIM, (h + 1) * HEAD_DIM)
        keys_all = jnp.concatenate([cache_local[:, 0, cols], new_keys[:, h]], axis=0)
        values_all = jnp.concatenate([cache_local[:, 1, cols], new_values[:, h]], axis=0)
        heads.append(attend(queries[:, h], keys_all, values_all, live, cache_slots))
    attended = jnp.concatenate(heads, axis=1)
    partial_out = jnp.dot(attended, out_cols, preferred_element_type=jnp.float32).astype(jnp.bfloat16)
    branch = lax.psum_scatter(partial_out, ("y", "c"), scatter_dimension=1, tiled=True)
    last_term = partial_out[new_rows - 1].reshape(n_y, n_c, n_zh, block_cols)
    last_term = jnp.transpose(last_term, (0, 2, 1, 3)).reshape(n_gx, block_cols)
    last_terms = lax.all_to_all(last_term, GX, 0, 0, tiled=True)
    last_row = (
        layer_input[new_rows - 1].astype(jnp.float32) + jnp.sum(last_terms.astype(jnp.float32), axis=0)
    ).astype(jnp.bfloat16)
    every_last = lax.all_to_all(
        jnp.broadcast_to(last_row[None], (n_gy, block_cols)), GY, 0, 0, tiled=True
    )
    last_wide = every_last.astype(jnp.float32)
    square_part = jnp.sum(last_wide * last_wide, axis=1, keepdims=True)
    gained = (last_wide * final_gain.astype(jnp.float32)).astype(jnp.bfloat16)
    logit_part = jnp.einsum("rd,vd->rv", gained, head_weight, preferred_element_type=jnp.float32)
    packed = jnp.concatenate([logit_part, square_part], axis=1)
    packed, branch = lax.optimization_barrier((packed, branch))
    branch = branch.reshape(new_rows, n_zh, block_cols)
    zh = lax.axis_index("zh")
    mine = lax.dynamic_index_in_dim(branch, zh, 1, keepdims=False)
    theirs = lax.dynamic_index_in_dim(branch, 1 - zh, 1, keepdims=False)
    from_partner = lax.ppermute(theirs, "zh", [(0, 1), (1, 0)])
    packed = lax.all_to_all(packed, GX, 0, 0, tiled=True)
    own_requests = packed.shape[0] // n_gx
    packed = jnp.sum(packed.reshape(n_gx, own_requests, packed.shape[1]), axis=0)
    vocab_part = logit_part.shape[1]
    logits = packed[:, :vocab_part] * lax.rsqrt(packed[:, vocab_part:] / D + 1e-06)
    stats = jnp.stack([jnp.sum(logits * logits, axis=1), jnp.max(logits, axis=1)], axis=0)
    spread = jnp.broadcast_to(stats[None], (n_gy,) + stats.shape)
    stats = lax.all_to_all(spread, GY, 0, 0, tiled=True)
    logit_scale = jnp.sqrt(jnp.sum(stats[:, 0], axis=0) / VOCAB)
    logit_peak = jnp.max(stats[:, 1], axis=0)

    layer_output = (
        layer_input.astype(jnp.float32) + mine.astype(jnp.float32) + from_partner.astype(jnp.float32)
    ).astype(jnp.bfloat16)
    return (layer_output, appended, logit_scale, logit_peak)


def solution(mesh):
    devices = np.asarray(mesh.devices)
    n_gx, n_gy = devices.shape
    fine = Mesh(devices.reshape(n_gx // 4, 2, 2, n_gy // 4, 4), GX + GY)
    return jax.shard_map(
        per_device,
        mesh=fine,
        in_specs=(
            P(GY, GX),
            P(None, None, GX),
            P(GX, None),
            P(GY, None, None, GX),
            P(),
            P(GX),
            P(GY, GX),
        ),
        out_specs=(P(GY, GX), P(GY, None, GX), P(GX), P(GX)),
        check_vma=False,
    )
```

```python
import functools

import jax
import jax.numpy as jnp
import numpy as np
from jax import lax
from jax.experimental import pallas as pl
from jax.experimental.pallas import tpu as pltpu
from jax.sharding import Mesh
from jax.sharding import PartitionSpec as P

D = 2048
HEAD_DIM = 128
VOCAB = 76032

NEG_FILL = -1e30

GX = ("y", "zh", "c")
GY = ("zl", "x")


def attention_kernel(cache_slots, key_rows, len_ref, q_ref, k_ref, v_ref, o_ref, m_sc, l_sc, acc_sc):
    step = pl.program_id(0)

    @pl.when(step == 0)
    def _():
        m_sc[...] = jnp.full(m_sc.shape, NEG_FILL, jnp.float32)
        l_sc[...] = jnp.zeros(l_sc.shape, jnp.float32)
        acc_sc[...] = jnp.zeros(acc_sc.shape, jnp.float32)

    q = q_ref[...]
    k = k_ref[...]
    s = lax.dot_general(q, k, (((1,), (1,)), ((), ())), preferred_element_type=jnp.float32) * HEAD_DIM ** (-0.5)
    rows = q.shape[0]
    slot = step * key_rows + lax.broadcasted_iota(jnp.int32, (rows, key_rows), 1)
    place = lax.broadcasted_iota(jnp.int32, (rows, key_rows), 0)
    limit = jnp.where(slot < cache_slots, len_ref[0], cache_slots + place + 1)
    allowed = slot < limit
    s = jnp.where(allowed, s, NEG_FILL)
    m_old = m_sc[...]
    m_new = jnp.maximum(m_old, jnp.max(s, axis=1, keepdims=True))
    p = jnp.where(allowed, jnp.exp(s - m_new), 0.0)
    factor = jnp.exp(m_old - m_new)
    l_sc[...] = l_sc[...] * factor + jnp.sum(p, axis=1, keepdims=True)
    v = v_ref[...]
    high = p.astype(jnp.bfloat16)
    low = (p - high.astype(jnp.float32)).astype(jnp.bfloat16)
    pv = jnp.dot(high, v, preferred_element_type=jnp.float32) + jnp.dot(low, v, preferred_element_type=jnp.float32)
    acc_sc[...] = acc_sc[...] * factor + pv
    m_sc[...] = m_new

    @pl.when(step == pl.num_programs(0) - 1)
    def _():
        o_ref[...] = (acc_sc[...] / l_sc[...]).astype(o_ref.dtype)


def attend(queries, keys, values, live_slots, cache_slots, key_rows=512):
    rows, width = queries.shape
    steps = keys.shape[0] // key_rows
    return pl.pallas_call(
        functools.partial(attention_kernel, cache_slots, key_rows),
        grid_spec=pltpu.PrefetchScalarGridSpec(
            num_scalar_prefetch=1,
            grid=(steps,),
            in_specs=[
                pl.BlockSpec((rows, width), lambda i, n: (0, 0)),
                pl.BlockSpec((key_rows, width), lambda i, n: (i, 0)),
                pl.BlockSpec((key_rows, width), lambda i, n: (i, 0)),
            ],
            out_specs=pl.BlockSpec((rows, width), lambda i, n: (0, 0)),
            scratch_shapes=[
                pltpu.VMEM((rows, 1), jnp.float32),
                pltpu.VMEM((rows, 1), jnp.float32),
                pltpu.VMEM((rows, width), jnp.float32),
            ],
        ),
        out_shape=jax.ShapeDtypeStruct((rows, width), jnp.bfloat16),
        compiler_params=pltpu.CompilerParams(dimension_semantics=("arbitrary",)),
    )(live_slots, queries, keys, values)


def per_device(
    layer_input,
    project_weight,
    output_weight,
    cache_entries,
    cached_lengths,
    final_gain,
    head_weight,
):
    new_rows, block_cols = layer_input.shape
    n_y, n_zh, n_c = lax.axis_size("y"), lax.axis_size("zh"), lax.axis_size("c")
    n_gx = n_y * n_zh * n_c
    n_gy = lax.axis_size("zl") * lax.axis_size("x")
    head_count = output_weight.shape[0] // HEAD_DIM
    request = lax.axis_index("zl") * lax.axis_size("x") + lax.axis_index("x")
    own_len = lax.dynamic_index_in_dim(cached_lengths, request, 0, keepdims=False)

    pair = lax.all_gather(layer_input, "zh", axis=1, tiled=True)
    features = lax.all_gather(pair, ("y", "c"), axis=1, tiled=True)
    weight_rows = project_weight.reshape(n_y, n_zh, n_c, block_cols, 3, project_weight.shape[-1])
    weight_rows = jnp.transpose(weight_rows, (0, 2, 1, 3, 4, 5)).reshape(project_weight.shape)

    widened = features.astype(jnp.float32)
    normed = (
        widened * lax.rsqrt(jnp.mean(widened * widened, axis=1, keepdims=True) + 1e-06)
    ).astype(jnp.bfloat16)
    projected = jnp.einsum(
        "td,dcf->tcf", normed, weight_rows, preferred_element_type=jnp.float32
    )
    rounded = projected.astype(jnp.bfloat16)
    queries = rounded[:, 0].reshape(new_rows, head_count, HEAD_DIM)
    new_keys = rounded[:, 1].reshape(new_rows, head_count, HEAD_DIM)
    new_values = rounded[:, 2].reshape(new_rows, head_count, HEAD_DIM)
    appended = rounded[:, 1:3]
    cache_local = cache_entries[0]

    out_cols = output_weight.reshape(-1, n_y, n_zh, n_c, block_cols)
    out_cols = jnp.transpose(out_cols, (0, 1, 3, 2, 4)).reshape(output_weight.shape)

    cache_slots = cache_local.shape[0]
    live = jnp.reshape(own_len, (1,)).astype(jnp.int32)
    heads = []
    for h in range(head_count):
        cols = slice(h * HEAD_DIM, (h + 1) * HEAD_DIM)
        keys_all = jnp.concatenate([cache_local[:, 0, cols], new_keys[:, h]], axis=0)
        values_all = jnp.concatenate([cache_local[:, 1, cols], new_values[:, h]], axis=0)
        heads.append(attend(queries[:, h], keys_all, values_all, live, cache_slots))
    attended = jnp.concatenate(heads, axis=1)
    partial_out = jnp.dot(attended, out_cols, preferred_element_type=jnp.float32).astype(jnp.bfloat16)
    branch = lax.psum_scatter(partial_out, ("y", "c"), scatter_dimension=1, tiled=True)
    last_term = partial_out[new_rows - 1].reshape(n_y, n_c, n_zh, block_cols)
    last_term = jnp.transpose(last_term, (0, 2, 1, 3)).reshape(n_gx, block_cols)
    last_terms = lax.all_to_all(last_term, GX, 0, 0, tiled=True)
    last_row = (
        layer_input[new_rows - 1].astype(jnp.float32) + jnp.sum(last_terms.astype(jnp.float32), axis=0)
    ).astype(jnp.bfloat16)
    every_last = lax.all_to_all(
        jnp.broadcast_to(last_row[None], (n_gy, block_cols)), GY, 0, 0, tiled=True
    )
    last_wide = every_last.astype(jnp.float32)
    square_part = jnp.sum(last_wide * last_wide, axis=1, keepdims=True)
    gained = (last_wide * final_gain.astype(jnp.float32)).astype(jnp.bfloat16)
    logit_part = jnp.einsum("rd,vd->rv", gained, head_weight, preferred_element_type=jnp.float32)
    packed = jnp.concatenate([logit_part, square_part], axis=1)
    packed, branch = lax.optimization_barrier((packed, branch))
    branch = lax.psum_scatter(branch, "zh", scatter_dimension=1, tiled=True)
    packed = lax.all_to_all(packed, GX, 0, 0, tiled=True)
    own_requests = packed.shape[0] // n_gx
    packed = jnp.sum(packed.reshape(n_gx, own_requests, packed.shape[1]), axis=0)
    vocab_part = logit_part.shape[1]
    logits = packed[:, :vocab_part] * lax.rsqrt(packed[:, vocab_part:] / D + 1e-06)
    stats = jnp.stack([jnp.sum(logits * logits, axis=1), jnp.max(logits, axis=1)], axis=0)
    spread = jnp.broadcast_to(stats[None], (n_gy,) + stats.shape)
    stats = lax.all_to_all(spread, GY, 0, 0, tiled=True)
    logit_scale = jnp.sqrt(jnp.sum(stats[:, 0], axis=0) / VOCAB)
    logit_peak = jnp.max(stats[:, 1], axis=0)

    branch, logit_scale, logit_peak = lax.optimization_barrier((branch, logit_scale, logit_peak))
    layer_output = (layer_input.astype(jnp.float32) + branch.astype(jnp.float32)).astype(jnp.bfloat16)
    return (layer_output, appended, logit_scale, logit_peak)


def solution(mesh):
    devices = np.asarray(mesh.devices)
    n_gx, n_gy = devices.shape
    fine = Mesh(devices.reshape(n_gx // 4, 2, 2, n_gy // 4, 4), GX + GY)
    return jax.shard_map(
        per_device,
        mesh=fine,
        in_specs=(
            P(GY, GX),
            P(None, None, GX),
            P(GX, None),
            P(GY, None, None, GX),
            P(),
            P(GX),
            P(GY, GX),
        ),
        out_specs=(P(GY, GX), P(GY, None, GX), P(GX), P(GX)),
        check_vma=False,
    )
```

```python
import functools

import jax
import jax.numpy as jnp
import numpy as np
from jax import lax
from jax.experimental import pallas as pl
from jax.experimental.pallas import tpu as pltpu
from jax.sharding import Mesh
from jax.sharding import PartitionSpec as P

D = 2048
HEAD_DIM = 128
VOCAB = 76032

NEG_FILL = -1e30

GX = ("y", "zh", "c")
GY = ("zl", "x")


def attention_kernel(cache_slots, key_rows, len_ref, q_ref, k_ref, v_ref, o_ref, m_sc, l_sc, acc_sc):
    step = pl.program_id(0)

    @pl.when(step == 0)
    def _():
        m_sc[...] = jnp.full(m_sc.shape, NEG_FILL, jnp.float32)
        l_sc[...] = jnp.zeros(l_sc.shape, jnp.float32)
        acc_sc[...] = jnp.zeros(acc_sc.shape, jnp.float32)

    q = q_ref[...]
    k = k_ref[...]
    s = lax.dot_general(q, k, (((1,), (1,)), ((), ())), preferred_element_type=jnp.float32) * HEAD_DIM ** (-0.5)
    rows = q.shape[0]
    slot = step * key_rows + lax.broadcasted_iota(jnp.int32, (rows, key_rows), 1)
    place = lax.broadcasted_iota(jnp.int32, (rows, key_rows), 0)
    limit = jnp.where(slot < cache_slots, len_ref[0], cache_slots + place + 1)
    allowed = slot < limit
    s = jnp.where(allowed, s, NEG_FILL)
    m_old = m_sc[...]
    m_new = jnp.maximum(m_old, jnp.max(s, axis=1, keepdims=True))
    p = jnp.where(allowed, jnp.exp(s - m_new), 0.0)
    factor = jnp.exp(m_old - m_new)
    l_sc[...] = l_sc[...] * factor + jnp.sum(p, axis=1, keepdims=True)
    v = v_ref[...]
    high = p.astype(jnp.bfloat16)
    low = (p - high.astype(jnp.float32)).astype(jnp.bfloat16)
    pv = jnp.dot(high, v, preferred_element_type=jnp.float32) + jnp.dot(low, v, preferred_element_type=jnp.float32)
    acc_sc[...] = acc_sc[...] * factor + pv
    m_sc[...] = m_new

    @pl.when(step == pl.num_programs(0) - 1)
    def _():
        o_ref[...] = (acc_sc[...] / l_sc[...]).astype(o_ref.dtype)


def attend(queries, keys, values, live_slots, cache_slots, key_rows=512):
    rows, width = queries.shape
    steps = keys.shape[0] // key_rows
    return pl.pallas_call(
        functools.partial(attention_kernel, cache_slots, key_rows),
        grid_spec=pltpu.PrefetchScalarGridSpec(
            num_scalar_prefetch=1,
            grid=(steps,),
            in_specs=[
                pl.BlockSpec((rows, width), lambda i, n: (0, 0)),
                pl.BlockSpec((key_rows, width), lambda i, n: (i, 0)),
                pl.BlockSpec((key_rows, width), lambda i, n: (i, 0)),
            ],
            out_specs=pl.BlockSpec((rows, width), lambda i, n: (0, 0)),
            scratch_shapes=[
                pltpu.VMEM((rows, 1), jnp.float32),
                pltpu.VMEM((rows, 1), jnp.float32),
                pltpu.VMEM((rows, width), jnp.float32),
            ],
        ),
        out_shape=jax.ShapeDtypeStruct((rows, width), jnp.bfloat16),
        compiler_params=pltpu.CompilerParams(dimension_semantics=("arbitrary",)),
    )(live_slots, queries, keys, values)


def per_device(
    layer_input,
    project_weight,
    output_weight,
    cache_entries,
    cached_lengths,
    final_gain,
    head_weight,
):
    new_rows, block_cols = layer_input.shape
    n_y, n_zh, n_c = lax.axis_size("y"), lax.axis_size("zh"), lax.axis_size("c")
    n_gx = n_y * n_zh * n_c
    n_gy = lax.axis_size("zl") * lax.axis_size("x")
    head_count = output_weight.shape[0] // HEAD_DIM
    request = lax.axis_index("zl") * lax.axis_size("x") + lax.axis_index("x")
    own_len = lax.dynamic_index_in_dim(cached_lengths, request, 0, keepdims=False)

    pair = lax.all_gather(layer_input, "zh", axis=1, tiled=True)
    features = lax.all_gather(pair, ("y", "c"), axis=1, tiled=True)
    weight_rows = project_weight.reshape(n_y, n_zh, n_c, block_cols, 3, project_weight.shape[-1])
    weight_rows = jnp.transpose(weight_rows, (0, 2, 1, 3, 4, 5)).reshape(project_weight.shape)

    widened = features.astype(jnp.float32)
    normed = (
        widened * lax.rsqrt(jnp.mean(widened * widened, axis=1, keepdims=True) + 1e-06)
    ).astype(jnp.bfloat16)
    projected = jnp.einsum(
        "td,dcf->tcf", normed, weight_rows, preferred_element_type=jnp.float32
    )
    rounded = projected.astype(jnp.bfloat16)
    queries = rounded[:, 0].reshape(new_rows, head_count, HEAD_DIM)
    new_keys = rounded[:, 1].reshape(new_rows, head_count, HEAD_DIM)
    new_values = rounded[:, 2].reshape(new_rows, head_count, HEAD_DIM)
    appended = rounded[:, 1:3]
    cache_local = cache_entries[0]

    out_cols = output_weight.reshape(-1, n_y, n_zh, n_c, block_cols)
    out_cols = jnp.transpose(out_cols, (0, 1, 3, 2, 4)).reshape(output_weight.shape)
    partner_cols = lax.ppermute(out_cols, "zh", [(0, 1), (1, 0)])

    cache_slots = cache_local.shape[0]
    live = jnp.reshape(own_len, (1,)).astype(jnp.int32)
    heads = []
    for h in range(head_count):
        cols = slice(h * HEAD_DIM, (h + 1) * HEAD_DIM)
        keys_all = jnp.concatenate([cache_local[:, 0, cols], new_keys[:, h]], axis=0)
        values_all = jnp.concatenate([cache_local[:, 1, cols], new_values[:, h]], axis=0)
        heads.append(attend(queries[:, h], keys_all, values_all, live, cache_slots))
    attended = jnp.concatenate(heads, axis=1)
    pair = [(0, 1), (1, 0)]
    partner_attended = lax.ppermute(attended, "zh", pair)
    partial_out = jnp.dot(attended, out_cols, preferred_element_type=jnp.float32).astype(jnp.bfloat16)
    last_term = partial_out[new_rows - 1].reshape(n_y, n_c, n_zh, block_cols)
    last_term = jnp.transpose(last_term, (0, 2, 1, 3)).reshape(n_gx, block_cols)
    last_terms = lax.all_to_all(last_term, GX, 0, 0, tiled=True)
    partner_attended, last_terms = lax.optimization_barrier((partner_attended, last_terms))
    partner_out = jnp.dot(partner_attended, partner_cols, preferred_element_type=jnp.float32).astype(jnp.bfloat16)
    pair_out = (partial_out.astype(jnp.float32) + partner_out.astype(jnp.float32)).astype(jnp.bfloat16)
    branch = lax.psum_scatter(pair_out, ("y", "c"), scatter_dimension=1, tiled=True)
    branch = lax.dynamic_index_in_dim(
        branch.reshape(new_rows, n_zh, block_cols), lax.axis_index("zh"), 1, keepdims=False
    )
    last_row = (
        layer_input[new_rows - 1].astype(jnp.float32) + jnp.sum(last_terms.astype(jnp.float32), axis=0)
    ).astype(jnp.bfloat16)
    every_last = lax.all_to_all(
        jnp.broadcast_to(last_row[None], (n_gy, block_cols)), GY, 0, 0, tiled=True
    )
    last_wide = every_last.astype(jnp.float32)
    square_part = jnp.sum(last_wide * last_wide, axis=1, keepdims=True)
    gained = (last_wide * final_gain.astype(jnp.float32)).astype(jnp.bfloat16)
    logit_part = jnp.einsum("rd,vd->rv", gained, head_weight, preferred_element_type=jnp.float32)
    packed = jnp.concatenate([logit_part, square_part], axis=1)
    packed = lax.all_to_all(packed, GX, 0, 0, tiled=True)
    own_requests = packed.shape[0] // n_gx
    packed = jnp.sum(packed.reshape(n_gx, own_requests, packed.shape[1]), axis=0)
    vocab_part = logit_part.shape[1]
    logits = packed[:, :vocab_part] * lax.rsqrt(packed[:, vocab_part:] / D + 1e-06)
    stats = jnp.stack([jnp.sum(logits * logits, axis=1), jnp.max(logits, axis=1)], axis=0)
    spread = jnp.broadcast_to(stats[None], (n_gy,) + stats.shape)
    stats = lax.all_to_all(spread, GY, 0, 0, tiled=True)
    logit_scale = jnp.sqrt(jnp.sum(stats[:, 0], axis=0) / VOCAB)
    logit_peak = jnp.max(stats[:, 1], axis=0)

    branch, logit_scale, logit_peak = lax.optimization_barrier((branch, logit_scale, logit_peak))
    layer_output = (layer_input.astype(jnp.float32) + branch.astype(jnp.float32)).astype(jnp.bfloat16)
    return (layer_output, appended, logit_scale, logit_peak)


def solution(mesh):
    devices = np.asarray(mesh.devices)
    n_gx, n_gy = devices.shape
    fine = Mesh(devices.reshape(n_gx // 4, 2, 2, n_gy // 4, 4), GX + GY)
    return jax.shard_map(
        per_device,
        mesh=fine,
        in_specs=(
            P(GY, GX),
            P(None, None, GX),
            P(GX, None),
            P(GY, None, None, GX),
            P(),
            P(GX),
            P(GY, GX),
        ),
        out_specs=(P(GY, GX), P(GY, None, GX), P(GX), P(GX)),
        check_vma=False,
    )
```

```python
import functools

import jax
import jax.numpy as jnp
import numpy as np
from jax import lax
from jax.experimental import pallas as pl
from jax.experimental.pallas import tpu as pltpu
from jax.sharding import Mesh
from jax.sharding import PartitionSpec as P

D = 2048
HEAD_DIM = 128
VOCAB = 76032

NEG_FILL = -1e30

GX = ("y", "zh", "c")
GY = ("zl", "x")


def attention_kernel(cache_slots, key_rows, len_ref, q_ref, k_ref, v_ref, o_ref, m_sc, l_sc, acc_sc):
    step = pl.program_id(0)

    @pl.when(step == 0)
    def _():
        m_sc[...] = jnp.full(m_sc.shape, NEG_FILL, jnp.float32)
        l_sc[...] = jnp.zeros(l_sc.shape, jnp.float32)
        acc_sc[...] = jnp.zeros(acc_sc.shape, jnp.float32)

    q = q_ref[...]
    k = k_ref[...]
    s = lax.dot_general(q, k, (((1,), (1,)), ((), ())), preferred_element_type=jnp.float32) * HEAD_DIM ** (-0.5)
    rows = q.shape[0]
    slot = step * key_rows + lax.broadcasted_iota(jnp.int32, (rows, key_rows), 1)
    place = lax.broadcasted_iota(jnp.int32, (rows, key_rows), 0)
    limit = jnp.where(slot < cache_slots, len_ref[0], cache_slots + place + 1)
    allowed = slot < limit
    s = jnp.where(allowed, s, NEG_FILL)
    m_old = m_sc[...]
    m_new = jnp.maximum(m_old, jnp.max(s, axis=1, keepdims=True))
    p = jnp.where(allowed, jnp.exp(s - m_new), 0.0)
    factor = jnp.exp(m_old - m_new)
    l_sc[...] = l_sc[...] * factor + jnp.sum(p, axis=1, keepdims=True)
    v = v_ref[...]
    high = p.astype(jnp.bfloat16)
    low = (p - high.astype(jnp.float32)).astype(jnp.bfloat16)
    pv = jnp.dot(high, v, preferred_element_type=jnp.float32) + jnp.dot(low, v, preferred_element_type=jnp.float32)
    acc_sc[...] = acc_sc[...] * factor + pv
    m_sc[...] = m_new

    @pl.when(step == pl.num_programs(0) - 1)
    def _():
        o_ref[...] = (acc_sc[...] / l_sc[...]).astype(o_ref.dtype)


def attend(queries, keys, values, live_slots, cache_slots, key_rows=512):
    rows, width = queries.shape
    steps = keys.shape[0] // key_rows
    return pl.pallas_call(
        functools.partial(attention_kernel, cache_slots, key_rows),
        grid_spec=pltpu.PrefetchScalarGridSpec(
            num_scalar_prefetch=1,
            grid=(steps,),
            in_specs=[
                pl.BlockSpec((rows, width), lambda i, n: (0, 0)),
                pl.BlockSpec((key_rows, width), lambda i, n: (i, 0)),
                pl.BlockSpec((key_rows, width), lambda i, n: (i, 0)),
            ],
            out_specs=pl.BlockSpec((rows, width), lambda i, n: (0, 0)),
            scratch_shapes=[
                pltpu.VMEM((rows, 1), jnp.float32),
                pltpu.VMEM((rows, 1), jnp.float32),
                pltpu.VMEM((rows, width), jnp.float32),
            ],
        ),
        out_shape=jax.ShapeDtypeStruct((rows, width), jnp.bfloat16),
        compiler_params=pltpu.CompilerParams(dimension_semantics=("arbitrary",)),
    )(live_slots, queries, keys, values)


def per_device(
    layer_input,
    project_weight,
    output_weight,
    cache_entries,
    cached_lengths,
    final_gain,
    head_weight,
):
    new_rows, block_cols = layer_input.shape
    n_y, n_zh, n_c = lax.axis_size("y"), lax.axis_size("zh"), lax.axis_size("c")
    n_gx = n_y * n_zh * n_c
    n_gy = lax.axis_size("zl") * lax.axis_size("x")
    head_count = output_weight.shape[0] // HEAD_DIM
    request = lax.axis_index("zl") * lax.axis_size("x") + lax.axis_index("x")
    own_len = lax.dynamic_index_in_dim(cached_lengths, request, 0, keepdims=False)

    pair = lax.all_gather(layer_input, "zh", axis=1, tiled=True)
    features = lax.all_gather(pair, ("y", "c"), axis=1, tiled=True)
    weight_rows = project_weight.reshape(n_y, n_zh, n_c, block_cols, 3, project_weight.shape[-1])
    weight_rows = jnp.transpose(weight_rows, (0, 2, 1, 3, 4, 5)).reshape(project_weight.shape)

    widened = features.astype(jnp.float32)
    normed = (
        widened * lax.rsqrt(jnp.mean(widened * widened, axis=1, keepdims=True) + 1e-06)
    ).astype(jnp.bfloat16)
    projected = jnp.einsum(
        "td,dcf->tcf", normed, weight_rows, preferred_element_type=jnp.float32
    )
    rounded = projected.astype(jnp.bfloat16)
    queries = rounded[:, 0].reshape(new_rows, head_count, HEAD_DIM)
    new_keys = rounded[:, 1].reshape(new_rows, head_count, HEAD_DIM)
    new_values = rounded[:, 2].reshape(new_rows, head_count, HEAD_DIM)
    appended = rounded[:, 1:3]
    cache_local = cache_entries[0]

    out_cols = output_weight.reshape(-1, n_y, n_zh, n_c, block_cols)
    out_cols = jnp.transpose(out_cols, (0, 1, 3, 2, 4)).reshape(output_weight.shape)

    cache_slots = cache_local.shape[0]
    live = jnp.reshape(own_len, (1,)).astype(jnp.int32)
    heads = []
    for h in range(head_count):
        cols = slice(h * HEAD_DIM, (h + 1) * HEAD_DIM)
        keys_all = jnp.concatenate([cache_local[:, 0, cols], new_keys[:, h]], axis=0)
        values_all = jnp.concatenate([cache_local[:, 1, cols], new_values[:, h]], axis=0)
        heads.append(attend(queries[:, h], keys_all, values_all, live, cache_slots))
    attended = jnp.concatenate(heads, axis=1)
    partial_out = jnp.dot(attended, out_cols, preferred_element_type=jnp.float32).astype(jnp.bfloat16)
    branch = lax.psum_scatter(partial_out, ("y", "c"), scatter_dimension=1, tiled=True)
    last_term = partial_out[new_rows - 1].reshape(n_y, n_c, n_zh, block_cols)
    last_term = jnp.transpose(last_term, (0, 2, 1, 3)).reshape(n_gx, block_cols)
    own_block = (lax.axis_index(GX) == jnp.arange(n_gx))[:, None]
    terms = last_term.astype(jnp.float32) + jnp.where(
        own_block, layer_input[new_rows - 1].astype(jnp.float32)[None], 0.0
    )
    spread = jnp.broadcast_to(terms[:, None], (n_gx, n_gy, block_cols)).reshape(n_gx * n_gy, block_cols)
    rows_in = lax.all_to_all(spread, GX + GY, 0, 0, tiled=True)
    every_last = jnp.sum(rows_in.reshape(n_gx, n_gy, block_cols), axis=0).astype(jnp.bfloat16)
    last_wide = every_last.astype(jnp.float32)
    square_part = jnp.sum(last_wide * last_wide, axis=1, keepdims=True)
    gained = (last_wide * final_gain.astype(jnp.float32)).astype(jnp.bfloat16)
    logit_part = jnp.einsum("rd,vd->rv", gained, head_weight, preferred_element_type=jnp.float32)
    packed = jnp.concatenate([logit_part, square_part], axis=1)
    packed, branch = lax.optimization_barrier((packed, branch))
    branch = lax.psum_scatter(branch, "zh", scatter_dimension=1, tiled=True)
    packed = lax.all_to_all(packed, GX, 0, 0, tiled=True)
    own_requests = packed.shape[0] // n_gx
    packed = jnp.sum(packed.reshape(n_gx, own_requests, packed.shape[1]), axis=0)
    vocab_part = logit_part.shape[1]
    logits = packed[:, :vocab_part] * lax.rsqrt(packed[:, vocab_part:] / D + 1e-06)
    stats = jnp.stack([jnp.sum(logits * logits, axis=1), jnp.max(logits, axis=1)], axis=0)
    spread = jnp.broadcast_to(stats[None], (n_gy,) + stats.shape)
    stats = lax.all_to_all(spread, GY, 0, 0, tiled=True)
    logit_scale = jnp.sqrt(jnp.sum(stats[:, 0], axis=0) / VOCAB)
    logit_peak = jnp.max(stats[:, 1], axis=0)

    branch, logit_scale, logit_peak = lax.optimization_barrier((branch, logit_scale, logit_peak))
    layer_output = (layer_input.astype(jnp.float32) + branch.astype(jnp.float32)).astype(jnp.bfloat16)
    return (layer_output, appended, logit_scale, logit_peak)


def solution(mesh):
    devices = np.asarray(mesh.devices)
    n_gx, n_gy = devices.shape
    fine = Mesh(devices.reshape(n_gx // 4, 2, 2, n_gy // 4, 4), GX + GY)
    return jax.shard_map(
        per_device,
        mesh=fine,
        in_specs=(
            P(GY, GX),
            P(None, None, GX),
            P(GX, None),
            P(GY, None, None, GX),
            P(),
            P(GX),
            P(GY, GX),
        ),
        out_specs=(P(GY, GX), P(GY, None, GX), P(GX), P(GX)),
        check_vma=False,
    )
```

```python
import functools

import jax
import jax.numpy as jnp
import numpy as np
from jax import lax
from jax.experimental import pallas as pl
from jax.experimental.pallas import tpu as pltpu
from jax.sharding import Mesh
from jax.sharding import PartitionSpec as P

D = 2048
HEAD_DIM = 128
VOCAB = 76032

NEG_FILL = -1e30

GX = ("y", "zh", "c")
GY = ("zl", "x")


def attention_kernel(cache_blocks, key_rows, len_ref, q_ref, kc_ref, vc_ref, kn_ref, vn_ref, o_ref, m_sc, l_sc, acc_sc):
    step = pl.program_id(0)
    cache_slots = cache_blocks * key_rows

    @pl.when(step == 0)
    def _():
        m_sc[...] = jnp.full(m_sc.shape, NEG_FILL, jnp.float32)
        l_sc[...] = jnp.zeros(l_sc.shape, jnp.float32)
        acc_sc[...] = jnp.zeros(acc_sc.shape, jnp.float32)

    def fold(k, v):
        q = q_ref[...]
        s = lax.dot_general(q, k, (((1,), (1,)), ((), ())), preferred_element_type=jnp.float32) * HEAD_DIM ** (-0.5)
        rows = q.shape[0]
        slot = step * key_rows + lax.broadcasted_iota(jnp.int32, (rows, key_rows), 1)
        place = lax.broadcasted_iota(jnp.int32, (rows, key_rows), 0)
        limit = jnp.where(slot < cache_slots, len_ref[0], cache_slots + place + 1)
        allowed = slot < limit
        s = jnp.where(allowed, s, NEG_FILL)
        m_old = m_sc[...]
        m_new = jnp.maximum(m_old, jnp.max(s, axis=1, keepdims=True))
        p = jnp.where(allowed, jnp.exp(s - m_new), 0.0)
        factor = jnp.exp(m_old - m_new)
        l_sc[...] = l_sc[...] * factor + jnp.sum(p, axis=1, keepdims=True)
        high = p.astype(jnp.bfloat16)
        low = (p - high.astype(jnp.float32)).astype(jnp.bfloat16)
        pv = jnp.dot(high, v, preferred_element_type=jnp.float32) + jnp.dot(low, v, preferred_element_type=jnp.float32)
        acc_sc[...] = acc_sc[...] * factor + pv
        m_sc[...] = m_new

    @pl.when(step < cache_blocks)
    def _():
        fold(kc_ref[...], vc_ref[...])

    @pl.when(step == cache_blocks)
    def _():
        fold(kn_ref[...], vn_ref[...])
        o_ref[...] = (acc_sc[...] / l_sc[...]).astype(o_ref.dtype)


def attend(queries, cache_keys, cache_values, new_keys, new_values, live_slots):
    rows, width = queries.shape
    cache_blocks = cache_keys.shape[0] // rows
    last = cache_blocks - 1
    return pl.pallas_call(
        functools.partial(attention_kernel, cache_blocks, rows),
        grid_spec=pltpu.PrefetchScalarGridSpec(
            num_scalar_prefetch=1,
            grid=(cache_blocks + 1,),
            in_specs=[
                pl.BlockSpec((rows, width), lambda i, n: (0, 0)),
                pl.BlockSpec((rows, width), lambda i, n: (jnp.minimum(i, last), 0)),
                pl.BlockSpec((rows, width), lambda i, n: (jnp.minimum(i, last), 0)),
                pl.BlockSpec((rows, width), lambda i, n: (0, 0)),
                pl.BlockSpec((rows, width), lambda i, n: (0, 0)),
            ],
            out_specs=pl.BlockSpec((rows, width), lambda i, n: (0, 0)),
            scratch_shapes=[
                pltpu.VMEM((rows, 1), jnp.float32),
                pltpu.VMEM((rows, 1), jnp.float32),
                pltpu.VMEM((rows, width), jnp.float32),
            ],
        ),
        out_shape=jax.ShapeDtypeStruct((rows, width), jnp.bfloat16),
        compiler_params=pltpu.CompilerParams(dimension_semantics=("arbitrary",)),
    )(live_slots, queries, cache_keys, cache_values, new_keys, new_values)


def per_device(
    layer_input,
    project_weight,
    output_weight,
    cache_entries,
    cached_lengths,
    final_gain,
    head_weight,
):
    new_rows, block_cols = layer_input.shape
    n_y, n_zh, n_c = lax.axis_size("y"), lax.axis_size("zh"), lax.axis_size("c")
    n_gx = n_y * n_zh * n_c
    n_gy = lax.axis_size("zl") * lax.axis_size("x")
    head_count = output_weight.shape[0] // HEAD_DIM
    request = lax.axis_index("zl") * lax.axis_size("x") + lax.axis_index("x")
    own_len = lax.dynamic_index_in_dim(cached_lengths, request, 0, keepdims=False)

    pair = lax.all_gather(layer_input, "zh", axis=1, tiled=True)
    features = lax.all_gather(pair, ("y", "c"), axis=1, tiled=True)
    weight_rows = project_weight.reshape(n_y, n_zh, n_c, block_cols, 3, project_weight.shape[-1])
    weight_rows = jnp.transpose(weight_rows, (0, 2, 1, 3, 4, 5)).reshape(project_weight.shape)

    widened = features.astype(jnp.float32)
    normed = (
        widened * lax.rsqrt(jnp.mean(widened * widened, axis=1, keepdims=True) + 1e-06)
    ).astype(jnp.bfloat16)
    projected = jnp.einsum(
        "td,dcf->tcf", normed, weight_rows, preferred_element_type=jnp.float32
    )
    rounded = projected.astype(jnp.bfloat16)
    queries = rounded[:, 0].reshape(new_rows, head_count, HEAD_DIM)
    new_keys = rounded[:, 1].reshape(new_rows, head_count, HEAD_DIM)
    new_values = rounded[:, 2].reshape(new_rows, head_count, HEAD_DIM)
    appended = rounded[:, 1:3]
    cache_local = cache_entries[0]

    out_cols = output_weight.reshape(-1, n_y, n_zh, n_c, block_cols)
    out_cols = jnp.transpose(out_cols, (0, 1, 3, 2, 4)).reshape(output_weight.shape)

    cache_slots = cache_local.shape[0]
    live = jnp.reshape(own_len, (1,)).astype(jnp.int32)
    heads = []
    for h in range(head_count):
        cols = slice(h * HEAD_DIM, (h + 1) * HEAD_DIM)
        heads.append(attend(
            queries[:, h], cache_local[:, 0, cols], cache_local[:, 1, cols], new_keys[:, h], new_values[:, h], live
        ))
    attended = jnp.concatenate(heads, axis=1)
    partial_out = jnp.dot(attended, out_cols, preferred_element_type=jnp.float32).astype(jnp.bfloat16)
    branch = lax.psum_scatter(partial_out, ("y", "c"), scatter_dimension=1, tiled=True)
    last_term = partial_out[new_rows - 1].reshape(n_y, n_c, n_zh, block_cols)
    last_term = jnp.transpose(last_term, (0, 2, 1, 3)).reshape(n_gx, block_cols)
    last_terms = lax.all_to_all(last_term, GX, 0, 0, tiled=True)
    last_row = (
        layer_input[new_rows - 1].astype(jnp.float32) + jnp.sum(last_terms.astype(jnp.float32), axis=0)
    ).astype(jnp.bfloat16)
    every_last = lax.all_to_all(
        jnp.broadcast_to(last_row[None], (n_gy, block_cols)), GY, 0, 0, tiled=True
    )
    last_wide = every_last.astype(jnp.float32)
    square_part = jnp.sum(last_wide * last_wide, axis=1, keepdims=True)
    gained = (last_wide * final_gain.astype(jnp.float32)).astype(jnp.bfloat16)
    logit_part = jnp.einsum("rd,vd->rv", gained, head_weight, preferred_element_type=jnp.float32)
    packed = jnp.concatenate([logit_part, square_part], axis=1)
    packed, branch = lax.optimization_barrier((packed, branch))
    branch = lax.psum_scatter(branch, "zh", scatter_dimension=1, tiled=True)
    packed = lax.all_to_all(packed, GX, 0, 0, tiled=True)
    own_requests = packed.shape[0] // n_gx
    packed = jnp.sum(packed.reshape(n_gx, own_requests, packed.shape[1]), axis=0)
    vocab_part = logit_part.shape[1]
    logits = packed[:, :vocab_part] * lax.rsqrt(packed[:, vocab_part:] / D + 1e-06)
    stats = jnp.stack([jnp.sum(logits * logits, axis=1), jnp.max(logits, axis=1)], axis=0)
    spread = jnp.broadcast_to(stats[None], (n_gy,) + stats.shape)
    stats = lax.all_to_all(spread, GY, 0, 0, tiled=True)
    logit_scale = jnp.sqrt(jnp.sum(stats[:, 0], axis=0) / VOCAB)
    logit_peak = jnp.max(stats[:, 1], axis=0)

    branch, logit_scale, logit_peak = lax.optimization_barrier((branch, logit_scale, logit_peak))
    layer_output = (layer_input.astype(jnp.float32) + branch.astype(jnp.float32)).astype(jnp.bfloat16)
    return (layer_output, appended, logit_scale, logit_peak)


def solution(mesh):
    devices = np.asarray(mesh.devices)
    n_gx, n_gy = devices.shape
    fine = Mesh(devices.reshape(n_gx // 4, 2, 2, n_gy // 4, 4), GX + GY)
    return jax.shard_map(
        per_device,
        mesh=fine,
        in_specs=(
            P(GY, GX),
            P(None, None, GX),
            P(GX, None),
            P(GY, None, None, GX),
            P(),
            P(GX),
            P(GY, GX),
        ),
        out_specs=(P(GY, GX), P(GY, None, GX), P(GX), P(GX)),
        check_vma=False,
    )
```

```python
import functools

import jax
import jax.numpy as jnp
import numpy as np
from jax import lax
from jax.experimental import pallas as pl
from jax.experimental.pallas import tpu as pltpu
from jax.sharding import Mesh
from jax.sharding import PartitionSpec as P

D = 2048
HEAD_DIM = 128
VOCAB = 76032

NEG_FILL = -1e30

GX = ("y", "zh", "c")
GY = ("zl", "x")


def attention_kernel(cache_blocks, key_rows, len_ref, q_ref, kc_ref, vc_ref, kn_ref, vn_ref, o_ref, m_sc, l_sc, acc_sc):
    step = pl.program_id(0)
    cache_slots = cache_blocks * key_rows

    @pl.when(step == 0)
    def _():
        m_sc[...] = jnp.full(m_sc.shape, NEG_FILL, jnp.float32)
        l_sc[...] = jnp.zeros(l_sc.shape, jnp.float32)
        acc_sc[...] = jnp.zeros(acc_sc.shape, jnp.float32)

    def fold(k, v, limit):
        q = q_ref[...]
        s = lax.dot_general(q, k, (((1,), (1,)), ((), ())), preferred_element_type=jnp.float32) * HEAD_DIM ** (-0.5)
        if limit is not None:
            rows = q.shape[0]
            slot = step * key_rows + lax.broadcasted_iota(jnp.int32, (rows, key_rows), 1)
            allowed = slot < limit(rows)
            s = jnp.where(allowed, s, NEG_FILL)
        m_old = m_sc[...]
        m_new = jnp.maximum(m_old, jnp.max(s, axis=1, keepdims=True))
        p = jnp.exp(s - m_new)
        if limit is not None:
            p = jnp.where(allowed, p, 0.0)
        factor = jnp.exp(m_old - m_new)
        l_sc[...] = l_sc[...] * factor + jnp.sum(p, axis=1, keepdims=True)
        high = p.astype(jnp.bfloat16)
        low = (p - high.astype(jnp.float32)).astype(jnp.bfloat16)
        pv = jnp.dot(high, v, preferred_element_type=jnp.float32) + jnp.dot(low, v, preferred_element_type=jnp.float32)
        acc_sc[...] = acc_sc[...] * factor + pv
        m_sc[...] = m_new

    live = len_ref[0]
    first_slot = step * key_rows
    in_cache = step < cache_blocks

    @pl.when(in_cache & (first_slot + key_rows <= live))
    def _():
        fold(kc_ref[...], vc_ref[...], None)

    @pl.when(in_cache & (first_slot < live) & (first_slot + key_rows > live))
    def _():
        fold(kc_ref[...], vc_ref[...], lambda rows: live)

    @pl.when(step == cache_blocks)
    def _():
        fold(
            kn_ref[...],
            vn_ref[...],
            lambda rows: cache_slots + lax.broadcasted_iota(jnp.int32, (rows, key_rows), 0) + 1,
        )
        o_ref[...] = (acc_sc[...] / l_sc[...]).astype(o_ref.dtype)


def attend(queries, cache_keys, cache_values, new_keys, new_values, live_slots):
    rows, width = queries.shape
    cache_blocks = cache_keys.shape[0] // rows
    last = cache_blocks - 1
    return pl.pallas_call(
        functools.partial(attention_kernel, cache_blocks, rows),
        grid_spec=pltpu.PrefetchScalarGridSpec(
            num_scalar_prefetch=1,
            grid=(cache_blocks + 1,),
            in_specs=[
                pl.BlockSpec((rows, width), lambda i, n: (0, 0)),
                pl.BlockSpec((rows, width), lambda i, n: (jnp.minimum(i, last), 0)),
                pl.BlockSpec((rows, width), lambda i, n: (jnp.minimum(i, last), 0)),
                pl.BlockSpec((rows, width), lambda i, n: (0, 0)),
                pl.BlockSpec((rows, width), lambda i, n: (0, 0)),
            ],
            out_specs=pl.BlockSpec((rows, width), lambda i, n: (0, 0)),
            scratch_shapes=[
                pltpu.VMEM((rows, 1), jnp.float32),
                pltpu.VMEM((rows, 1), jnp.float32),
                pltpu.VMEM((rows, width), jnp.float32),
            ],
        ),
        out_shape=jax.ShapeDtypeStruct((rows, width), jnp.bfloat16),
        compiler_params=pltpu.CompilerParams(dimension_semantics=("arbitrary",)),
    )(live_slots, queries, cache_keys, cache_values, new_keys, new_values)


def per_device(
    layer_input,
    project_weight,
    output_weight,
    cache_entries,
    cached_lengths,
    final_gain,
    head_weight,
):
    new_rows, block_cols = layer_input.shape
    n_y, n_zh, n_c = lax.axis_size("y"), lax.axis_size("zh"), lax.axis_size("c")
    n_gx = n_y * n_zh * n_c
    n_gy = lax.axis_size("zl") * lax.axis_size("x")
    head_count = output_weight.shape[0] // HEAD_DIM
    request = lax.axis_index("zl") * lax.axis_size("x") + lax.axis_index("x")
    own_len = lax.dynamic_index_in_dim(cached_lengths, request, 0, keepdims=False)

    pair = lax.all_gather(layer_input, "zh", axis=1, tiled=True)
    features = lax.all_gather(pair, ("y", "c"), axis=1, tiled=True)
    weight_rows = project_weight.reshape(n_y, n_zh, n_c, block_cols, 3, project_weight.shape[-1])
    weight_rows = jnp.transpose(weight_rows, (0, 2, 1, 3, 4, 5)).reshape(project_weight.shape)

    widened = features.astype(jnp.float32)
    normed = (
        widened * lax.rsqrt(jnp.mean(widened * widened, axis=1, keepdims=True) + 1e-06)
    ).astype(jnp.bfloat16)
    projected = jnp.einsum(
        "td,dcf->tcf", normed, weight_rows, preferred_element_type=jnp.float32
    )
    rounded = projected.astype(jnp.bfloat16)
    queries = rounded[:, 0].reshape(new_rows, head_count, HEAD_DIM)
    new_keys = rounded[:, 1].reshape(new_rows, head_count, HEAD_DIM)
    new_values = rounded[:, 2].reshape(new_rows, head_count, HEAD_DIM)
    appended = rounded[:, 1:3]
    cache_local = cache_entries[0]

    out_cols = output_weight.reshape(-1, n_y, n_zh, n_c, block_cols)
    out_cols = jnp.transpose(out_cols, (0, 1, 3, 2, 4)).reshape(output_weight.shape)

    cache_slots = cache_local.shape[0]
    live = jnp.reshape(own_len, (1,)).astype(jnp.int32)
    heads = []
    for h in range(head_count):
        cols = slice(h * HEAD_DIM, (h + 1) * HEAD_DIM)
        heads.append(attend(
            queries[:, h], cache_local[:, 0, cols], cache_local[:, 1, cols], new_keys[:, h], new_values[:, h], live
        ))
    attended = jnp.concatenate(heads, axis=1)
    partial_out = jnp.dot(attended, out_cols, preferred_element_type=jnp.float32).astype(jnp.bfloat16)
    branch = lax.psum_scatter(partial_out, ("y", "c"), scatter_dimension=1, tiled=True)
    last_term = partial_out[new_rows - 1].reshape(n_y, n_c, n_zh, block_cols)
    last_term = jnp.transpose(last_term, (0, 2, 1, 3)).reshape(n_gx, block_cols)
    last_terms = lax.all_to_all(last_term, GX, 0, 0, tiled=True)
    last_row = (
        layer_input[new_rows - 1].astype(jnp.float32) + jnp.sum(last_terms.astype(jnp.float32), axis=0)
    ).astype(jnp.bfloat16)
    every_last = lax.all_to_all(
        jnp.broadcast_to(last_row[None], (n_gy, block_cols)), GY, 0, 0, tiled=True
    )
    last_wide = every_last.astype(jnp.float32)
    square_part = jnp.sum(last_wide * last_wide, axis=1, keepdims=True)
    gained = (last_wide * final_gain.astype(jnp.float32)).astype(jnp.bfloat16)
    logit_part = jnp.einsum("rd,vd->rv", gained, head_weight, preferred_element_type=jnp.float32)
    packed = jnp.concatenate([logit_part, square_part], axis=1)
    packed, branch = lax.optimization_barrier((packed, branch))
    branch = lax.psum_scatter(branch, "zh", scatter_dimension=1, tiled=True)
    packed = lax.all_to_all(packed, GX, 0, 0, tiled=True)
    own_requests = packed.shape[0] // n_gx
    packed = jnp.sum(packed.reshape(n_gx, own_requests, packed.shape[1]), axis=0)
    vocab_part = logit_part.shape[1]
    logits = packed[:, :vocab_part] * lax.rsqrt(packed[:, vocab_part:] / D + 1e-06)
    stats = jnp.stack([jnp.sum(logits * logits, axis=1), jnp.max(logits, axis=1)], axis=0)
    spread = jnp.broadcast_to(stats[None], (n_gy,) + stats.shape)
    stats = lax.all_to_all(spread, GY, 0, 0, tiled=True)
    logit_scale = jnp.sqrt(jnp.sum(stats[:, 0], axis=0) / VOCAB)
    logit_peak = jnp.max(stats[:, 1], axis=0)

    branch, logit_scale, logit_peak = lax.optimization_barrier((branch, logit_scale, logit_peak))
    layer_output = (layer_input.astype(jnp.float32) + branch.astype(jnp.float32)).astype(jnp.bfloat16)
    return (layer_output, appended, logit_scale, logit_peak)


def solution(mesh):
    devices = np.asarray(mesh.devices)
    n_gx, n_gy = devices.shape
    fine = Mesh(devices.reshape(n_gx // 4, 2, 2, n_gy // 4, 4), GX + GY)
    return jax.shard_map(
        per_device,
        mesh=fine,
        in_specs=(
            P(GY, GX),
            P(None, None, GX),
            P(GX, None),
            P(GY, None, None, GX),
            P(),
            P(GX),
            P(GY, GX),
        ),
        out_specs=(P(GY, GX), P(GY, None, GX), P(GX), P(GX)),
        check_vma=False,
    )
```

```python
import functools

import jax
import jax.numpy as jnp
import numpy as np
from jax import lax
from jax.experimental import pallas as pl
from jax.experimental.pallas import tpu as pltpu
from jax.sharding import Mesh
from jax.sharding import PartitionSpec as P

D = 2048
HEAD_DIM = 128
VOCAB = 76032

NEG_FILL = -1e30

GX = ("y", "zh", "c")
GY = ("zl", "x")


def attention_kernel(cache_blocks, key_rows, len_ref, q_ref, kc_ref, vc_ref, kn_ref, vn_ref, o_ref, m_sc, l_sc, acc_sc):
    step = pl.program_id(0)
    cache_slots = cache_blocks * key_rows

    @pl.when(step == 0)
    def _():
        m_sc[...] = jnp.full(m_sc.shape, NEG_FILL, jnp.float32)
        l_sc[...] = jnp.zeros(l_sc.shape, jnp.float32)
        acc_sc[...] = jnp.zeros(acc_sc.shape, jnp.float32)

    def fold(k, v, limit):
        q = q_ref[...]
        s = lax.dot_general(q, k, (((1,), (1,)), ((), ())), preferred_element_type=jnp.float32) * HEAD_DIM ** (-0.5)
        if limit is not None:
            rows = q.shape[0]
            slot = step * key_rows + lax.broadcasted_iota(jnp.int32, (rows, key_rows), 1)
            allowed = slot < limit(rows)
            s = jnp.where(allowed, s, NEG_FILL)
        m_old = m_sc[...]
        m_new = jnp.maximum(m_old, jnp.max(s, axis=1, keepdims=True))
        p = jnp.exp(s - m_new)
        if limit is not None:
            p = jnp.where(allowed, p, 0.0)
        factor = jnp.exp(m_old - m_new)
        l_sc[...] = l_sc[...] * factor + jnp.sum(p, axis=1, keepdims=True)
        high = p.astype(jnp.bfloat16)
        low = (p - high.astype(jnp.float32)).astype(jnp.bfloat16)
        pv = jnp.dot(high, v, preferred_element_type=jnp.float32) + jnp.dot(low, v, preferred_element_type=jnp.float32)
        acc_sc[...] = acc_sc[...] * factor + pv
        m_sc[...] = m_new

    live = len_ref[0]
    first_slot = step * key_rows
    in_cache = step < cache_blocks

    @pl.when(in_cache & (first_slot + key_rows <= live))
    def _():
        fold(kc_ref[...], vc_ref[...], None)

    @pl.when(in_cache & (first_slot < live) & (first_slot + key_rows > live))
    def _():
        fold(kc_ref[...], vc_ref[...], lambda rows: live)

    @pl.when(step == cache_blocks)
    def _():
        fold(
            kn_ref[...],
            vn_ref[...],
            lambda rows: cache_slots + lax.broadcasted_iota(jnp.int32, (rows, key_rows), 0) + 1,
        )
        o_ref[...] = (acc_sc[...] / l_sc[...]).astype(o_ref.dtype)


def attend(queries, cache_keys, cache_values, new_keys, new_values, live_slots):
    rows, width = queries.shape
    cache_blocks = cache_keys.shape[0] // rows
    last = cache_blocks - 1
    return pl.pallas_call(
        functools.partial(attention_kernel, cache_blocks, rows),
        grid_spec=pltpu.PrefetchScalarGridSpec(
            num_scalar_prefetch=1,
            grid=(cache_blocks + 1,),
            in_specs=[
                pl.BlockSpec((rows, width), lambda i, n: (0, 0)),
                pl.BlockSpec((rows, width), lambda i, n: (jnp.minimum(i, last), 0)),
                pl.BlockSpec((rows, width), lambda i, n: (jnp.minimum(i, last), 0)),
                pl.BlockSpec((rows, width), lambda i, n: (0, 0)),
                pl.BlockSpec((rows, width), lambda i, n: (0, 0)),
            ],
            out_specs=pl.BlockSpec((rows, width), lambda i, n: (0, 0)),
            scratch_shapes=[
                pltpu.VMEM((rows, 1), jnp.float32),
                pltpu.VMEM((rows, 1), jnp.float32),
                pltpu.VMEM((rows, width), jnp.float32),
            ],
        ),
        out_shape=jax.ShapeDtypeStruct((rows, width), jnp.bfloat16),
        compiler_params=pltpu.CompilerParams(dimension_semantics=("arbitrary",)),
    )(live_slots, queries, cache_keys, cache_values, new_keys, new_values)


def per_device(
    layer_input,
    project_weight,
    output_weight,
    cache_entries,
    cached_lengths,
    final_gain,
    head_weight,
):
    new_rows, block_cols = layer_input.shape
    n_y, n_zh, n_c = lax.axis_size("y"), lax.axis_size("zh"), lax.axis_size("c")
    n_gx = n_y * n_zh * n_c
    n_gy = lax.axis_size("zl") * lax.axis_size("x")
    head_count = output_weight.shape[0] // HEAD_DIM
    request = lax.axis_index("zl") * lax.axis_size("x") + lax.axis_index("x")
    own_len = lax.dynamic_index_in_dim(cached_lengths, request, 0, keepdims=False)

    pair = lax.all_gather(layer_input, "zh", axis=1, tiled=True)
    features = lax.all_gather(pair, ("y", "c"), axis=1, tiled=True)
    weight_rows = project_weight.reshape(n_y, n_zh, n_c, block_cols, 3, project_weight.shape[-1])
    weight_rows = jnp.transpose(weight_rows, (0, 2, 1, 3, 4, 5)).reshape(project_weight.shape)

    widened = features.astype(jnp.float32)
    normed = (
        widened * lax.rsqrt(jnp.mean(widened * widened, axis=1, keepdims=True) + 1e-06)
    ).astype(jnp.bfloat16)
    projected = jnp.einsum(
        "td,dcf->tcf", normed, weight_rows, preferred_element_type=jnp.float32
    )
    rounded = projected.astype(jnp.bfloat16)
    queries = rounded[:, 0].reshape(new_rows, head_count, HEAD_DIM)
    new_keys = rounded[:, 1].reshape(new_rows, head_count, HEAD_DIM)
    new_values = rounded[:, 2].reshape(new_rows, head_count, HEAD_DIM)
    appended = rounded[:, 1:3]
    cache_local = cache_entries[0]

    out_cols = output_weight.reshape(-1, n_y, n_zh, n_c, block_cols)
    out_cols = jnp.transpose(out_cols, (0, 1, 3, 2, 4)).reshape(output_weight.shape)

    cache_slots = cache_local.shape[0]
    live = jnp.reshape(own_len, (1,)).astype(jnp.int32)
    heads = []
    for h in range(head_count):
        cols = slice(h * HEAD_DIM, (h + 1) * HEAD_DIM)
        heads.append(attend(
            queries[:, h], cache_local[:, 0, cols], cache_local[:, 1, cols], new_keys[:, h], new_values[:, h], live
        ))
    attended = jnp.concatenate(heads, axis=1)
    partial_out = jnp.dot(attended, out_cols, preferred_element_type=jnp.float32).astype(jnp.bfloat16)
    branch = lax.psum_scatter(partial_out, ("y", "c"), scatter_dimension=1, tiled=True)
    last_term = partial_out[new_rows - 1].reshape(n_y, n_c, n_zh, block_cols)
    last_term = jnp.transpose(last_term, (0, 2, 1, 3)).reshape(n_gx, block_cols)
    own_block = (lax.axis_index(GX) == jnp.arange(n_gx))[:, None]
    terms = last_term.astype(jnp.float32) + jnp.where(
        own_block, layer_input[new_rows - 1].astype(jnp.float32)[None], 0.0
    )
    spread = jnp.broadcast_to(terms[:, None], (n_gx, n_gy, block_cols)).reshape(n_gx * n_gy, block_cols)
    rows_in = lax.all_to_all(spread, GX + GY, 0, 0, tiled=True)
    every_last = jnp.sum(rows_in.reshape(n_gx, n_gy, block_cols), axis=0).astype(jnp.bfloat16)
    last_wide = every_last.astype(jnp.float32)
    square_part = jnp.sum(last_wide * last_wide, axis=1, keepdims=True)
    gained = (last_wide * final_gain.astype(jnp.float32)).astype(jnp.bfloat16)
    logit_part = jnp.einsum("rd,vd->rv", gained, head_weight, preferred_element_type=jnp.float32)
    packed = jnp.concatenate([logit_part, square_part], axis=1)
    packed, branch = lax.optimization_barrier((packed, branch))
    branch = lax.psum_scatter(branch, "zh", scatter_dimension=1, tiled=True)
    packed = lax.all_to_all(packed, GX, 0, 0, tiled=True)
    own_requests = packed.shape[0] // n_gx
    packed = jnp.sum(packed.reshape(n_gx, own_requests, packed.shape[1]), axis=0)
    vocab_part = logit_part.shape[1]
    logits = packed[:, :vocab_part] * lax.rsqrt(packed[:, vocab_part:] / D + 1e-06)
    stats = jnp.stack([jnp.sum(logits * logits, axis=1), jnp.max(logits, axis=1)], axis=0)
    spread = jnp.broadcast_to(stats[None], (n_gy,) + stats.shape)
    stats = lax.all_to_all(spread, GY, 0, 0, tiled=True)
    logit_scale = jnp.sqrt(jnp.sum(stats[:, 0], axis=0) / VOCAB)
    logit_peak = jnp.max(stats[:, 1], axis=0)

    branch, logit_scale, logit_peak = lax.optimization_barrier((branch, logit_scale, logit_peak))
    layer_output = (layer_input.astype(jnp.float32) + branch.astype(jnp.float32)).astype(jnp.bfloat16)
    return (layer_output, appended, logit_scale, logit_peak)


def solution(mesh):
    devices = np.asarray(mesh.devices)
    n_gx, n_gy = devices.shape
    fine = Mesh(devices.reshape(n_gx // 4, 2, 2, n_gy // 4, 4), GX + GY)
    return jax.shard_map(
        per_device,
        mesh=fine,
        in_specs=(
            P(GY, GX),
            P(None, None, GX),
            P(GX, None),
            P(GY, None, None, GX),
            P(),
            P(GX),
            P(GY, GX),
        ),
        out_specs=(P(GY, GX), P(GY, None, GX), P(GX), P(GX)),
        check_vma=False,
    )
```

```python
import functools

import jax
import jax.numpy as jnp
import numpy as np
from jax import lax
from jax.experimental import pallas as pl
from jax.experimental.pallas import tpu as pltpu
from jax.sharding import Mesh
from jax.sharding import PartitionSpec as P

D = 2048
HEAD_DIM = 128
VOCAB = 76032

NEG_FILL = -1e30

GX = ("y", "zh", "c")
GY = ("zl", "x")


def attention_kernel(cache_blocks, key_rows, len_ref, q_ref, kc_ref, vc_ref, kn_ref, vn_ref, o_ref, m_sc, l_sc, acc_sc):
    step = pl.program_id(0)
    cache_slots = cache_blocks * key_rows

    @pl.when(step == 0)
    def _():
        m_sc[...] = jnp.full(m_sc.shape, NEG_FILL, jnp.float32)
        l_sc[...] = jnp.zeros(l_sc.shape, jnp.float32)
        acc_sc[...] = jnp.zeros(acc_sc.shape, jnp.float32)

    def fold(k, v, limit):
        q = q_ref[...]
        s = lax.dot_general(q, k, (((1,), (1,)), ((), ())), preferred_element_type=jnp.float32) * HEAD_DIM ** (-0.5)
        if limit is not None:
            rows = q.shape[0]
            slot = step * key_rows + lax.broadcasted_iota(jnp.int32, (rows, key_rows), 1)
            allowed = slot < limit(rows)
            s = jnp.where(allowed, s, NEG_FILL)
        m_old = m_sc[...]
        m_new = jnp.maximum(m_old, jnp.max(s, axis=1, keepdims=True))
        p = jnp.exp(s - m_new)
        if limit is not None:
            p = jnp.where(allowed, p, 0.0)
        factor = jnp.exp(m_old - m_new)
        l_sc[...] = l_sc[...] * factor + jnp.sum(p, axis=1, keepdims=True)
        high = p.astype(jnp.bfloat16)
        low = (p - high.astype(jnp.float32)).astype(jnp.bfloat16)
        pv = jnp.dot(high, v, preferred_element_type=jnp.float32) + jnp.dot(low, v, preferred_element_type=jnp.float32)
        acc_sc[...] = acc_sc[...] * factor + pv
        m_sc[...] = m_new

    live = len_ref[0]
    first_slot = step * key_rows
    in_cache = step < cache_blocks

    @pl.when(in_cache & (first_slot + key_rows <= live))
    def _():
        fold(kc_ref[...], vc_ref[...], None)

    @pl.when(in_cache & (first_slot < live) & (first_slot + key_rows > live))
    def _():
        fold(kc_ref[...], vc_ref[...], lambda rows: live)

    @pl.when(step == cache_blocks)
    def _():
        fold(
            kn_ref[...],
            vn_ref[...],
            lambda rows: cache_slots + lax.broadcasted_iota(jnp.int32, (rows, key_rows), 0) + 1,
        )
        o_ref[...] = (acc_sc[...] / l_sc[...]).astype(o_ref.dtype)


def attend(queries, cache_keys, cache_values, new_keys, new_values, live_slots):
    rows, width = queries.shape
    cache_blocks = cache_keys.shape[0] // rows
    last = cache_blocks - 1
    return pl.pallas_call(
        functools.partial(attention_kernel, cache_blocks, rows),
        grid_spec=pltpu.PrefetchScalarGridSpec(
            num_scalar_prefetch=1,
            grid=(cache_blocks + 1,),
            in_specs=[
                pl.BlockSpec((rows, width), lambda i, n: (0, 0)),
                pl.BlockSpec((rows, width), lambda i, n: (jnp.minimum(i, last), 0)),
                pl.BlockSpec((rows, width), lambda i, n: (jnp.minimum(i, last), 0)),
                pl.BlockSpec((rows, width), lambda i, n: (0, 0)),
                pl.BlockSpec((rows, width), lambda i, n: (0, 0)),
            ],
            out_specs=pl.BlockSpec((rows, width), lambda i, n: (0, 0)),
            scratch_shapes=[
                pltpu.VMEM((rows, 1), jnp.float32),
                pltpu.VMEM((rows, 1), jnp.float32),
                pltpu.VMEM((rows, width), jnp.float32),
            ],
        ),
        out_shape=jax.ShapeDtypeStruct((rows, width), jnp.bfloat16),
        compiler_params=pltpu.CompilerParams(dimension_semantics=("arbitrary",)),
    )(live_slots, queries, cache_keys, cache_values, new_keys, new_values)


def per_device(
    layer_input,
    project_weight,
    output_weight,
    cache_entries,
    cached_lengths,
    final_gain,
    head_weight,
):
    new_rows, block_cols = layer_input.shape
    n_y, n_zh, n_c = lax.axis_size("y"), lax.axis_size("zh"), lax.axis_size("c")
    n_gx = n_y * n_zh * n_c
    n_gy = lax.axis_size("zl") * lax.axis_size("x")
    head_count = output_weight.shape[0] // HEAD_DIM
    request = lax.axis_index("zl") * lax.axis_size("x") + lax.axis_index("x")
    own_len = lax.dynamic_index_in_dim(cached_lengths, request, 0, keepdims=False)

    half = lax.all_gather(layer_input, ("y", "c"), axis=1, tiled=True)
    features = lax.all_gather(half, "zh", axis=1, tiled=True)
    weight_rows = project_weight.reshape(n_y, n_zh, n_c, block_cols, 3, project_weight.shape[-1])
    weight_rows = jnp.transpose(weight_rows, (1, 0, 2, 3, 4, 5)).reshape(project_weight.shape)

    widened = features.astype(jnp.float32)
    normed = (
        widened * lax.rsqrt(jnp.mean(widened * widened, axis=1, keepdims=True) + 1e-06)
    ).astype(jnp.bfloat16)
    projected = jnp.einsum(
        "td,dcf->tcf", normed, weight_rows, preferred_element_type=jnp.float32
    )
    rounded = projected.astype(jnp.bfloat16)
    queries = rounded[:, 0].reshape(new_rows, head_count, HEAD_DIM)
    new_keys = rounded[:, 1].reshape(new_rows, head_count, HEAD_DIM)
    new_values = rounded[:, 2].reshape(new_rows, head_count, HEAD_DIM)
    appended = rounded[:, 1:3]
    cache_local = cache_entries[0]

    out_cols = output_weight.reshape(-1, n_y, n_zh, n_c, block_cols)
    out_cols = jnp.transpose(out_cols, (0, 1, 3, 2, 4)).reshape(output_weight.shape)

    cache_slots = cache_local.shape[0]
    live = jnp.reshape(own_len, (1,)).astype(jnp.int32)
    heads = []
    for h in range(head_count):
        cols = slice(h * HEAD_DIM, (h + 1) * HEAD_DIM)
        heads.append(attend(
            queries[:, h], cache_local[:, 0, cols], cache_local[:, 1, cols], new_keys[:, h], new_values[:, h], live
        ))
    attended = jnp.concatenate(heads, axis=1)
    partial_out = jnp.dot(attended, out_cols, preferred_element_type=jnp.float32).astype(jnp.bfloat16)
    branch = lax.psum_scatter(partial_out, ("y", "c"), scatter_dimension=1, tiled=True)
    last_term = partial_out[new_rows - 1].reshape(n_y, n_c, n_zh, block_cols)
    last_term = jnp.transpose(last_term, (0, 2, 1, 3)).reshape(n_gx, block_cols)
    last_terms = lax.all_to_all(last_term, GX, 0, 0, tiled=True)
    last_row = (
        layer_input[new_rows - 1].astype(jnp.float32) + jnp.sum(last_terms.astype(jnp.float32), axis=0)
    ).astype(jnp.bfloat16)
    every_last = lax.all_to_all(
        jnp.broadcast_to(last_row[None], (n_gy, block_cols)), GY, 0, 0, tiled=True
    )
    last_wide = every_last.astype(jnp.float32)
    square_part = jnp.sum(last_wide * last_wide, axis=1, keepdims=True)
    gained = (last_wide * final_gain.astype(jnp.float32)).astype(jnp.bfloat16)
    logit_part = jnp.einsum("rd,vd->rv", gained, head_weight, preferred_element_type=jnp.float32)
    packed = jnp.concatenate([logit_part, square_part], axis=1)
    packed, branch = lax.optimization_barrier((packed, branch))
    branch = lax.psum_scatter(branch, "zh", scatter_dimension=1, tiled=True)
    packed = lax.all_to_all(packed, GX, 0, 0, tiled=True)
    own_requests = packed.shape[0] // n_gx
    packed = jnp.sum(packed.reshape(n_gx, own_requests, packed.shape[1]), axis=0)
    vocab_part = logit_part.shape[1]
    logits = packed[:, :vocab_part] * lax.rsqrt(packed[:, vocab_part:] / D + 1e-06)
    stats = jnp.stack([jnp.sum(logits * logits, axis=1), jnp.max(logits, axis=1)], axis=0)
    spread = jnp.broadcast_to(stats[None], (n_gy,) + stats.shape)
    stats = lax.all_to_all(spread, GY, 0, 0, tiled=True)
    logit_scale = jnp.sqrt(jnp.sum(stats[:, 0], axis=0) / VOCAB)
    logit_peak = jnp.max(stats[:, 1], axis=0)

    branch, logit_scale, logit_peak = lax.optimization_barrier((branch, logit_scale, logit_peak))
    layer_output = (layer_input.astype(jnp.float32) + branch.astype(jnp.float32)).astype(jnp.bfloat16)
    return (layer_output, appended, logit_scale, logit_peak)


def solution(mesh):
    devices = np.asarray(mesh.devices)
    n_gx, n_gy = devices.shape
    fine = Mesh(devices.reshape(n_gx // 4, 2, 2, n_gy // 4, 4), GX + GY)
    return jax.shard_map(
        per_device,
        mesh=fine,
        in_specs=(
            P(GY, GX),
            P(None, None, GX),
            P(GX, None),
            P(GY, None, None, GX),
            P(),
            P(GX),
            P(GY, GX),
        ),
        out_specs=(P(GY, GX), P(GY, None, GX), P(GX), P(GX)),
        check_vma=False,
    )
```

```python
import functools

import jax
import jax.numpy as jnp
import numpy as np
from jax import lax
from jax.experimental import pallas as pl
from jax.experimental.pallas import tpu as pltpu
from jax.sharding import Mesh
from jax.sharding import PartitionSpec as P

D = 2048
HEAD_DIM = 128
VOCAB = 76032

NEG_FILL = -1e30

GX = ("y", "zh", "c")
GY = ("zl", "x")


def attention_kernel(cache_blocks, key_rows, new_rows, len_ref, q_ref, kc_ref, vc_ref, kn_ref, vn_ref, o_ref, m_sc, l_sc, acc_sc):
    step = pl.program_id(0)
    cache_slots = cache_blocks * key_rows

    @pl.when(step == 0)
    def _():
        m_sc[...] = jnp.full(m_sc.shape, NEG_FILL, jnp.float32)
        l_sc[...] = jnp.zeros(l_sc.shape, jnp.float32)
        acc_sc[...] = jnp.zeros(acc_sc.shape, jnp.float32)

    def fold(k, v, limit):
        q = q_ref[...]
        s = lax.dot_general(q, k, (((1,), (1,)), ((), ())), preferred_element_type=jnp.float32) * HEAD_DIM ** (-0.5)
        if limit is not None:
            rows, width = s.shape
            slot = step * key_rows + lax.broadcasted_iota(jnp.int32, (rows, width), 1)
            allowed = slot < limit(rows, width)
            s = jnp.where(allowed, s, NEG_FILL)
        m_old = m_sc[...]
        m_new = jnp.maximum(m_old, jnp.max(s, axis=1, keepdims=True))
        p = jnp.exp(s - m_new)
        if limit is not None:
            p = jnp.where(allowed, p, 0.0)
        factor = jnp.exp(m_old - m_new)
        l_sc[...] = l_sc[...] * factor + jnp.sum(p, axis=1, keepdims=True)
        high = p.astype(jnp.bfloat16)
        low = (p - high.astype(jnp.float32)).astype(jnp.bfloat16)
        pv = jnp.dot(high, v, preferred_element_type=jnp.float32) + jnp.dot(low, v, preferred_element_type=jnp.float32)
        acc_sc[...] = acc_sc[...] * factor + pv
        m_sc[...] = m_new

    live = len_ref[0]
    first_slot = step * key_rows
    in_cache = step < cache_blocks

    @pl.when(in_cache & (first_slot + key_rows <= live))
    def _():
        fold(kc_ref[...], vc_ref[...], None)

    @pl.when(in_cache & (first_slot < live) & (first_slot + key_rows > live))
    def _():
        fold(kc_ref[...], vc_ref[...], lambda rows, width: live)

    @pl.when(step == cache_blocks)
    def _():
        fold(
            kn_ref[...],
            vn_ref[...],
            lambda rows, width: cache_slots + lax.broadcasted_iota(jnp.int32, (rows, width), 0) + 1,
        )
        o_ref[...] = (acc_sc[...] / l_sc[...]).astype(o_ref.dtype)


def attend(queries, cache_keys, cache_values, new_keys, new_values, live_slots):
    rows, width = queries.shape
    key_rows = cache_keys.shape[0] // 4 if cache_keys.shape[0] % (4 * 128) == 0 else rows
    cache_blocks = cache_keys.shape[0] // key_rows
    last = cache_blocks - 1
    return pl.pallas_call(
        functools.partial(attention_kernel, cache_blocks, key_rows, rows),
        grid_spec=pltpu.PrefetchScalarGridSpec(
            num_scalar_prefetch=1,
            grid=(cache_blocks + 1,),
            in_specs=[
                pl.BlockSpec((rows, width), lambda i, n: (0, 0)),
                pl.BlockSpec((key_rows, width), lambda i, n: (jnp.minimum(i, last), 0)),
                pl.BlockSpec((key_rows, width), lambda i, n: (jnp.minimum(i, last), 0)),
                pl.BlockSpec((rows, width), lambda i, n: (0, 0)),
                pl.BlockSpec((rows, width), lambda i, n: (0, 0)),
            ],
            out_specs=pl.BlockSpec((rows, width), lambda i, n: (0, 0)),
            scratch_shapes=[
                pltpu.VMEM((rows, 1), jnp.float32),
                pltpu.VMEM((rows, 1), jnp.float32),
                pltpu.VMEM((rows, width), jnp.float32),
            ],
        ),
        out_shape=jax.ShapeDtypeStruct((rows, width), jnp.bfloat16),
        compiler_params=pltpu.CompilerParams(dimension_semantics=("arbitrary",)),
    )(live_slots, queries, cache_keys, cache_values, new_keys, new_values)


def per_device(
    layer_input,
    project_weight,
    output_weight,
    cache_entries,
    cached_lengths,
    final_gain,
    head_weight,
):
    new_rows, block_cols = layer_input.shape
    n_y, n_zh, n_c = lax.axis_size("y"), lax.axis_size("zh"), lax.axis_size("c")
    n_gx = n_y * n_zh * n_c
    n_gy = lax.axis_size("zl") * lax.axis_size("x")
    head_count = output_weight.shape[0] // HEAD_DIM
    request = lax.axis_index("zl") * lax.axis_size("x") + lax.axis_index("x")
    own_len = lax.dynamic_index_in_dim(cached_lengths, request, 0, keepdims=False)

    pair = lax.all_gather(layer_input, "zh", axis=1, tiled=True)
    features = lax.all_gather(pair, ("y", "c"), axis=1, tiled=True)
    weight_rows = project_weight.reshape(n_y, n_zh, n_c, block_cols, 3, project_weight.shape[-1])
    weight_rows = jnp.transpose(weight_rows, (0, 2, 1, 3, 4, 5)).reshape(project_weight.shape)

    widened = features.astype(jnp.float32)
    normed = (
        widened * lax.rsqrt(jnp.mean(widened * widened, axis=1, keepdims=True) + 1e-06)
    ).astype(jnp.bfloat16)
    projected = jnp.einsum(
        "td,dcf->tcf", normed, weight_rows, preferred_element_type=jnp.float32
    )
    rounded = projected.astype(jnp.bfloat16)
    queries = rounded[:, 0].reshape(new_rows, head_count, HEAD_DIM)
    new_keys = rounded[:, 1].reshape(new_rows, head_count, HEAD_DIM)
    new_values = rounded[:, 2].reshape(new_rows, head_count, HEAD_DIM)
    appended = rounded[:, 1:3]
    cache_local = cache_entries[0]

    out_cols = output_weight.reshape(-1, n_y, n_zh, n_c, block_cols)
    out_cols = jnp.transpose(out_cols, (0, 1, 3, 2, 4)).reshape(output_weight.shape)

    cache_slots = cache_local.shape[0]
    live = jnp.reshape(own_len, (1,)).astype(jnp.int32)
    heads = []
    for h in range(head_count):
        cols = slice(h * HEAD_DIM, (h + 1) * HEAD_DIM)
        heads.append(attend(
            queries[:, h], cache_local[:, 0, cols], cache_local[:, 1, cols], new_keys[:, h], new_values[:, h], live
        ))
    attended = jnp.concatenate(heads, axis=1)
    partial_out = jnp.dot(attended, out_cols, preferred_element_type=jnp.float32).astype(jnp.bfloat16)
    branch = lax.psum_scatter(partial_out, ("y", "c"), scatter_dimension=1, tiled=True)
    last_term = partial_out[new_rows - 1].reshape(n_y, n_c, n_zh, block_cols)
    last_term = jnp.transpose(last_term, (0, 2, 1, 3)).reshape(n_gx, block_cols)
    last_terms = lax.all_to_all(last_term, GX, 0, 0, tiled=True)
    last_row = (
        layer_input[new_rows - 1].astype(jnp.float32) + jnp.sum(last_terms.astype(jnp.float32), axis=0)
    ).astype(jnp.bfloat16)
    every_last = lax.all_to_all(
        jnp.broadcast_to(last_row[None], (n_gy, block_cols)), GY, 0, 0, tiled=True
    )
    last_wide = every_last.astype(jnp.float32)
    square_part = jnp.sum(last_wide * last_wide, axis=1, keepdims=True)
    gained = (last_wide * final_gain.astype(jnp.float32)).astype(jnp.bfloat16)
    logit_part = jnp.einsum("rd,vd->rv", gained, head_weight, preferred_element_type=jnp.float32)
    packed = jnp.concatenate([logit_part, square_part], axis=1)
    packed, branch = lax.optimization_barrier((packed, branch))
    branch = lax.psum_scatter(branch, "zh", scatter_dimension=1, tiled=True)
    packed = lax.all_to_all(packed, GX, 0, 0, tiled=True)
    own_requests = packed.shape[0] // n_gx
    packed = jnp.sum(packed.reshape(n_gx, own_requests, packed.shape[1]), axis=0)
    vocab_part = logit_part.shape[1]
    logits = packed[:, :vocab_part] * lax.rsqrt(packed[:, vocab_part:] / D + 1e-06)
    stats = jnp.stack([jnp.sum(logits * logits, axis=1), jnp.max(logits, axis=1)], axis=0)
    spread = jnp.broadcast_to(stats[None], (n_gy,) + stats.shape)
    stats = lax.all_to_all(spread, GY, 0, 0, tiled=True)
    logit_scale = jnp.sqrt(jnp.sum(stats[:, 0], axis=0) / VOCAB)
    logit_peak = jnp.max(stats[:, 1], axis=0)

    branch, logit_scale, logit_peak = lax.optimization_barrier((branch, logit_scale, logit_peak))
    layer_output = (layer_input.astype(jnp.float32) + branch.astype(jnp.float32)).astype(jnp.bfloat16)
    return (layer_output, appended, logit_scale, logit_peak)


def solution(mesh):
    devices = np.asarray(mesh.devices)
    n_gx, n_gy = devices.shape
    fine = Mesh(devices.reshape(n_gx // 4, 2, 2, n_gy // 4, 4), GX + GY)
    return jax.shard_map(
        per_device,
        mesh=fine,
        in_specs=(
            P(GY, GX),
            P(None, None, GX),
            P(GX, None),
            P(GY, None, None, GX),
            P(),
            P(GX),
            P(GY, GX),
        ),
        out_specs=(P(GY, GX), P(GY, None, GX), P(GX), P(GX)),
        check_vma=False,
    )
```

```python
import functools

import jax
import jax.numpy as jnp
import numpy as np
from jax import lax
from jax.experimental import pallas as pl
from jax.experimental.pallas import tpu as pltpu
from jax.sharding import Mesh
from jax.sharding import PartitionSpec as P

D = 2048
HEAD_DIM = 128
VOCAB = 76032

NEG_FILL = -1e30

GX = ("y", "zh", "c")
GY = ("zl", "x")


def attention_kernel(cache_blocks, key_rows, new_rows, len_ref, q_ref, kc_ref, vc_ref, kn_ref, vn_ref, o_ref, m_sc, l_sc, acc_sc):
    step = pl.program_id(0)
    cache_slots = cache_blocks * key_rows

    @pl.when(step == 0)
    def _():
        m_sc[...] = jnp.full(m_sc.shape, NEG_FILL, jnp.float32)
        l_sc[...] = jnp.zeros(l_sc.shape, jnp.float32)
        acc_sc[...] = jnp.zeros(acc_sc.shape, jnp.float32)

    def fold(k, v, limit):
        q = q_ref[...]
        s = lax.dot_general(q, k, (((1,), (1,)), ((), ())), preferred_element_type=jnp.float32) * HEAD_DIM ** (-0.5)
        if limit is not None:
            rows, width = s.shape
            slot = step * key_rows + lax.broadcasted_iota(jnp.int32, (rows, width), 1)
            allowed = slot < limit(rows, width)
            s = jnp.where(allowed, s, NEG_FILL)
        m_old = m_sc[...]
        m_new = jnp.maximum(m_old, jnp.max(s, axis=1, keepdims=True))
        p = jnp.exp(s - m_new)
        if limit is not None:
            p = jnp.where(allowed, p, 0.0)
        factor = jnp.exp(m_old - m_new)
        l_sc[...] = l_sc[...] * factor + jnp.sum(p, axis=1, keepdims=True)
        high = p.astype(jnp.bfloat16)
        low = (p - high.astype(jnp.float32)).astype(jnp.bfloat16)
        pv = jnp.dot(high, v, preferred_element_type=jnp.float32) + jnp.dot(low, v, preferred_element_type=jnp.float32)
        acc_sc[...] = acc_sc[...] * factor + pv
        m_sc[...] = m_new

    live = len_ref[0]
    first_slot = step * key_rows
    in_cache = step < cache_blocks

    @pl.when(in_cache & (first_slot + key_rows <= live))
    def _():
        fold(kc_ref[...], vc_ref[...], None)

    @pl.when(in_cache & (first_slot < live) & (first_slot + key_rows > live))
    def _():
        fold(kc_ref[...], vc_ref[...], lambda rows, width: live)

    @pl.when(step == cache_blocks)
    def _():
        fold(
            kn_ref[...],
            vn_ref[...],
            lambda rows, width: cache_slots + lax.broadcasted_iota(jnp.int32, (rows, width), 0) + 1,
        )
        o_ref[...] = (acc_sc[...] / l_sc[...]).astype(o_ref.dtype)


def attend(queries, cache_keys, cache_values, new_keys, new_values, live_slots):
    rows, width = queries.shape
    key_rows = cache_keys.shape[0] // 2 if cache_keys.shape[0] % (2 * 128) == 0 else rows
    cache_blocks = cache_keys.shape[0] // key_rows
    last = cache_blocks - 1
    return pl.pallas_call(
        functools.partial(attention_kernel, cache_blocks, key_rows, rows),
        grid_spec=pltpu.PrefetchScalarGridSpec(
            num_scalar_prefetch=1,
            grid=(cache_blocks + 1,),
            in_specs=[
                pl.BlockSpec((rows, width), lambda i, n: (0, 0)),
                pl.BlockSpec((key_rows, width), lambda i, n: (jnp.minimum(i, last), 0)),
                pl.BlockSpec((key_rows, width), lambda i, n: (jnp.minimum(i, last), 0)),
                pl.BlockSpec((rows, width), lambda i, n: (0, 0)),
                pl.BlockSpec((rows, width), lambda i, n: (0, 0)),
            ],
            out_specs=pl.BlockSpec((rows, width), lambda i, n: (0, 0)),
            scratch_shapes=[
                pltpu.VMEM((rows, 1), jnp.float32),
                pltpu.VMEM((rows, 1), jnp.float32),
                pltpu.VMEM((rows, width), jnp.float32),
            ],
        ),
        out_shape=jax.ShapeDtypeStruct((rows, width), jnp.bfloat16),
        compiler_params=pltpu.CompilerParams(dimension_semantics=("arbitrary",)),
    )(live_slots, queries, cache_keys, cache_values, new_keys, new_values)


def per_device(
    layer_input,
    project_weight,
    output_weight,
    cache_entries,
    cached_lengths,
    final_gain,
    head_weight,
):
    new_rows, block_cols = layer_input.shape
    n_y, n_zh, n_c = lax.axis_size("y"), lax.axis_size("zh"), lax.axis_size("c")
    n_gx = n_y * n_zh * n_c
    n_gy = lax.axis_size("zl") * lax.axis_size("x")
    head_count = output_weight.shape[0] // HEAD_DIM
    request = lax.axis_index("zl") * lax.axis_size("x") + lax.axis_index("x")
    own_len = lax.dynamic_index_in_dim(cached_lengths, request, 0, keepdims=False)

    pair = lax.all_gather(layer_input, "zh", axis=1, tiled=True)
    features = lax.all_gather(pair, ("y", "c"), axis=1, tiled=True)
    weight_rows = project_weight.reshape(n_y, n_zh, n_c, block_cols, 3, project_weight.shape[-1])
    weight_rows = jnp.transpose(weight_rows, (0, 2, 1, 3, 4, 5)).reshape(project_weight.shape)

    widened = features.astype(jnp.float32)
    normed = (
        widened * lax.rsqrt(jnp.mean(widened * widened, axis=1, keepdims=True) + 1e-06)
    ).astype(jnp.bfloat16)
    projected = jnp.einsum(
        "td,dcf->tcf", normed, weight_rows, preferred_element_type=jnp.float32
    )
    rounded = projected.astype(jnp.bfloat16)
    queries = rounded[:, 0].reshape(new_rows, head_count, HEAD_DIM)
    new_keys = rounded[:, 1].reshape(new_rows, head_count, HEAD_DIM)
    new_values = rounded[:, 2].reshape(new_rows, head_count, HEAD_DIM)
    appended = rounded[:, 1:3]
    cache_local = cache_entries[0]

    out_cols = output_weight.reshape(-1, n_y, n_zh, n_c, block_cols)
    out_cols = jnp.transpose(out_cols, (0, 1, 3, 2, 4)).reshape(output_weight.shape)

    cache_slots = cache_local.shape[0]
    live = jnp.reshape(own_len, (1,)).astype(jnp.int32)
    heads = []
    for h in range(head_count):
        cols = slice(h * HEAD_DIM, (h + 1) * HEAD_DIM)
        heads.append(attend(
            queries[:, h], cache_local[:, 0, cols], cache_local[:, 1, cols], new_keys[:, h], new_values[:, h], live
        ))
    attended = jnp.concatenate(heads, axis=1)
    partial_out = jnp.dot(attended, out_cols, preferred_element_type=jnp.float32).astype(jnp.bfloat16)
    branch = lax.psum_scatter(partial_out, ("y", "c"), scatter_dimension=1, tiled=True)
    last_term = partial_out[new_rows - 1].reshape(n_y, n_c, n_zh, block_cols)
    last_term = jnp.transpose(last_term, (0, 2, 1, 3)).reshape(n_gx, block_cols)
    last_terms = lax.all_to_all(last_term, GX, 0, 0, tiled=True)
    last_row = (
        layer_input[new_rows - 1].astype(jnp.float32) + jnp.sum(last_terms.astype(jnp.float32), axis=0)
    ).astype(jnp.bfloat16)
    every_last = lax.all_to_all(
        jnp.broadcast_to(last_row[None], (n_gy, block_cols)), GY, 0, 0, tiled=True
    )
    last_wide = every_last.astype(jnp.float32)
    square_part = jnp.sum(last_wide * last_wide, axis=1, keepdims=True)
    gained = (last_wide * final_gain.astype(jnp.float32)).astype(jnp.bfloat16)
    logit_part = jnp.einsum("rd,vd->rv", gained, head_weight, preferred_element_type=jnp.float32)
    packed = jnp.concatenate([logit_part, square_part], axis=1)
    packed, branch = lax.optimization_barrier((packed, branch))
    branch = lax.psum_scatter(branch, "zh", scatter_dimension=1, tiled=True)
    packed = lax.all_to_all(packed, GX, 0, 0, tiled=True)
    own_requests = packed.shape[0] // n_gx
    packed = jnp.sum(packed.reshape(n_gx, own_requests, packed.shape[1]), axis=0)
    vocab_part = logit_part.shape[1]
    logits = packed[:, :vocab_part] * lax.rsqrt(packed[:, vocab_part:] / D + 1e-06)
    stats = jnp.stack([jnp.sum(logits * logits, axis=1), jnp.max(logits, axis=1)], axis=0)
    spread = jnp.broadcast_to(stats[None], (n_gy,) + stats.shape)
    stats = lax.all_to_all(spread, GY, 0, 0, tiled=True)
    logit_scale = jnp.sqrt(jnp.sum(stats[:, 0], axis=0) / VOCAB)
    logit_peak = jnp.max(stats[:, 1], axis=0)

    branch, logit_scale, logit_peak = lax.optimization_barrier((branch, logit_scale, logit_peak))
    layer_output = (layer_input.astype(jnp.float32) + branch.astype(jnp.float32)).astype(jnp.bfloat16)
    return (layer_output, appended, logit_scale, logit_peak)


def solution(mesh):
    devices = np.asarray(mesh.devices)
    n_gx, n_gy = devices.shape
    fine = Mesh(devices.reshape(n_gx // 4, 2, 2, n_gy // 4, 4), GX + GY)
    return jax.shard_map(
        per_device,
        mesh=fine,
        in_specs=(
            P(GY, GX),
            P(None, None, GX),
            P(GX, None),
            P(GY, None, None, GX),
            P(),
            P(GX),
            P(GY, GX),
        ),
        out_specs=(P(GY, GX), P(GY, None, GX), P(GX), P(GX)),
        check_vma=False,
    )
```
